32 devices in a mesh: seq: 8 (over y, x, core), ch: 4 (over z).
Axes of the slice: x: 2, y: 2, z: 4, core: 2. Of those that a mesh axis runs over, the one named last changes fastest.
Arguments:
- inputs: bfloat16 [4096, 2048], P('seq', 'ch'), may hold values from -6 to 6
- gate_in: float32 [2048], P('ch'), may hold values from 0.25 to 2
- gate_out: float32 [2048], P('ch'), may hold values from 0.25 to 2
- first_blocks: bfloat16 [8, 512, 512], P('seq'), may hold values from -0.25 to 0.25
- second_blocks: bfloat16 [512, 8, 8], P('seq'), may hold values from -2 to 2
- channel_blocks: bfloat16 [4, 512, 512], P('ch'), may hold values from -0.25 to 0.25
- group_mix: bfloat16 [512, 4, 4], replicated, may hold values from -3 to 3
- cotangent: bfloat16 [4096, 2048], P('seq', 'ch'), may hold values from -6 to 6
Outputs:
- outputs: bfloat16 [4096, 2048], P('seq', 'ch')
- input_grad: bfloat16 [4096, 2048], P('seq', 'ch')
- channel_grad: float32 [4, 512, 512], P('ch', 'seq')
- block_grad: float32 [8, 512, 512], P('seq', 'ch')
The draws below stay inside these ranges and needn't reach their ends.
All inputs are finite; a program needn't handle non-finite values.
Results may differ from the reference program's by a relative error of at most 0.0072.
Values may be sent and summed in bfloat16 or wider, within the bound.
No kernel may reach another device: no remote copies, remote signals or barrier semaphores. Data moves between devices by JAX's collectives and lax.ppermute only.
A program may use at most 64 MiB of HBM per device.

```python
import jax
import jax.numpy as jnp

D = 2048
Q = 512
G = 4
P_SIZE = 8
L = 4096
J = 512


def level_of(rng, extent, cuts, least, largest):
    loudness, own = 1.0, jax.random.fold_in(rng, 6)
    for dim, blocks in cuts:
        heights = jnp.exp(jax.random.uniform(jax.random.fold_in(own, dim), (blocks,), jnp.float32, least / len(cuts), largest / len(cuts)))
        loudness = loudness * jnp.repeat(heights, extent[dim] // blocks).reshape([-1 if axis == dim else 1 for axis in range(len(extent))])
    return loudness


def noise(rng, dims, scale, limit, shards=(), held_as=jnp.bfloat16):
    result = jax.random.normal(rng, dims, jnp.float32) * scale
    if len(shards) > 0:
        result = level_of(rng, dims, shards, -0.22, 0.18) * result
    return jnp.clip(result, min=-limit, max=limit).astype(held_as)


def setup_inputs(seed: int = 0) -> dict:
    streams_of = jax.random.split(jax.random.key(seed), 9)
    inputs = noise(streams_of[0], (L, D), 1.0, 6.0, ((0, 8), (1, 4)))
    gate_in = jnp.clip(0.25 + 1.75 * jax.random.uniform(streams_of[1], (D,), jnp.float32) ** level_of(streams_of[1], (D,), ((0, 4),), -0.2, 0.2), 0.25, 2.0)
    gate_out = jnp.clip(0.25 + 1.75 * jax.random.uniform(streams_of[2], (D,), jnp.float32) ** level_of(streams_of[2], (D,), ((0, 4),), -0.2, 0.2), 0.25, 2.0)
    first_blocks = noise(streams_of[3], (P_SIZE, Q, Q), Q ** -0.5, 0.25, ((0, 8),))
    second_blocks = noise(streams_of[4], (Q, P_SIZE, P_SIZE), P_SIZE ** -0.5, 2.0, ((0, 8),))
    channel_blocks = noise(streams_of[5], (G, J, J), J ** -0.5, 0.25, ((0, 4),))
    group_mix = noise(streams_of[6], (J, G, G), G ** -0.5, 3.0)
    cotangent = noise(streams_of[7], (L, D), 1.0, 6.0, ((0, 8), (1, 4)))
    return {"inputs": inputs, "gate_in": gate_in, "gate_out": gate_out, "first_blocks": first_blocks, "second_blocks": second_blocks, "channel_blocks": channel_blocks, "group_mix": group_mix, "cotangent": cotangent}


def reference(inputs, gate_in, gate_out, first_blocks, second_blocks, channel_blocks, group_mix, cotangent):
    source = inputs.astype(jnp.float32)
    slope_in = jax.nn.sigmoid(gate_in * source)
    gated = (source * slope_in).astype(jnp.bfloat16)
    gated_cube = gated.astype(jnp.float32).reshape(P_SIZE, Q, D)
    first_f = first_blocks.astype(jnp.float32)
    second_f = second_blocks.astype(jnp.float32)
    chan_f = channel_blocks.astype(jnp.float32)
    mix_f = group_mix.astype(jnp.float32)
    mixed_first = jnp.einsum('acb,abd->acd', first_f, gated_cube).astype(jnp.bfloat16)
    mixed_second = jnp.einsum('cea,acd->ecd', second_f, mixed_first.astype(jnp.float32)).astype(jnp.bfloat16)
    second_f32 = mixed_second.astype(jnp.float32).reshape(L, D)
    slope_out = jax.nn.sigmoid(gate_out * source)
    hidden = (source + second_f32 * slope_out).astype(jnp.bfloat16)
    grouped = hidden.astype(jnp.float32).reshape(L, G, J)
    pre_act = jnp.einsum('rgj,gjk->rgk', grouped, chan_f)
    activated = jax.nn.gelu(pre_act).astype(jnp.bfloat16)
    added = jnp.einsum('rgk,kgh->rhk', activated.astype(jnp.float32), mix_f)
    outputs = (grouped + added).astype(jnp.bfloat16).reshape(L, D)
    upstream = cotangent.astype(jnp.float32).reshape(L, G, J)
    act_grad = jnp.einsum('rhk,kgh->rgk', upstream, mix_f).astype(jnp.bfloat16)
    pre_grad = jax.vjp(jax.nn.gelu, pre_act)[1](act_grad.astype(jnp.float32))[0].astype(jnp.bfloat16)
    pre_grad_f = pre_grad.astype(jnp.float32)
    hidden_grad = (upstream + jnp.einsum('rgk,gjk->rgj', pre_grad_f, chan_f)).astype(jnp.bfloat16)
    channel_grad = jnp.einsum('rgj,rgk->gjk', grouped, pre_grad_f)
    grad_flat = hidden_grad.astype(jnp.float32).reshape(L, D)
    gated_grad = (grad_flat * slope_out).astype(jnp.bfloat16).reshape(P_SIZE, Q, D)
    first_grad = jnp.einsum('cea,ecd->acd', second_f, gated_grad.astype(jnp.float32)).astype(jnp.bfloat16)
    first_grad_f = first_grad.astype(jnp.float32)
    block_grad = jnp.einsum('acd,abd->acb', first_grad_f, gated_cube)
    spread = jnp.einsum('acb,acd->abd', first_f, first_grad_f).reshape(L, D)
    input_grad = grad_flat + spread * (slope_in + gate_in * source * slope_in * (1.0 - slope_in))
    input_grad = input_grad + grad_flat * second_f32 * slope_out * (1.0 - slope_out) * gate_out
    return (outputs, input_grad.astype(jnp.bfloat16), channel_grad, block_grad)
```

```python
import jax
import jax.numpy as jnp
from jax import lax
from jax.sharding import PartitionSpec as P


def to_columns(values):
    n = lax.axis_size("seq")
    pieces = values.reshape(n, values.shape[1] // n, values.shape[2])
    return lax.all_to_all(pieces, "seq", split_axis=0, concat_axis=0, tiled=True)


def to_rows(values):
    back = lax.all_to_all(values, "seq", split_axis=0, concat_axis=0, tiled=True)
    return back.reshape(back.shape[0] * back.shape[1], back.shape[2])


def gather_groups(blocks):
    return lax.all_gather(blocks, "ch", axis=0, tiled=False)


def on_device(
    inputs, gate_in, gate_out, first_blocks, second_blocks, channel_blocks, group_mix, cotangent
):
    count_a = first_blocks.shape[0]
    length_q = first_blocks.shape[1]
    rows_local = inputs.shape[0]
    width_local = inputs.shape[1]
    groups_local = channel_blocks.shape[0]
    block_width = channel_blocks.shape[1]
    me = lax.axis_index("ch")
    mix_f = group_mix.astype(jnp.float32)
    mix_out = lax.dynamic_index_in_dim(mix_f, me, axis=2, keepdims=False)
    mix_back = lax.dynamic_index_in_dim(mix_f, me, axis=1, keepdims=False)

    upstream = cotangent.reshape(rows_local, groups_local, block_width)
    every_upstream = gather_groups(cotangent).astype(jnp.float32)
    act_grad = jnp.einsum("hrk,kh->rk", every_upstream, mix_back).astype(jnp.bfloat16)
    act_grad = act_grad.reshape(rows_local, groups_local, block_width)

    source = inputs.astype(jnp.float32).reshape(count_a, length_q, width_local)
    slope_in = jax.nn.sigmoid(gate_in * source)
    gated = (source * slope_in).astype(jnp.bfloat16)
    mixed_first = jnp.einsum(
        "acb,abd->acd", first_blocks, gated, preferred_element_type=jnp.float32
    ).astype(jnp.bfloat16)
    turned = to_columns(mixed_first)
    mixed_second = jnp.einsum(
        "cea,acd->ecd", second_blocks, turned, preferred_element_type=jnp.float32
    ).astype(jnp.bfloat16)
    returned = to_rows(mixed_second).astype(jnp.float32).reshape(count_a, length_q, width_local)
    slope_out = jax.nn.sigmoid(gate_out * source)
    hidden = (source + returned * slope_out).astype(jnp.bfloat16)
    grouped = hidden.reshape(rows_local, groups_local, block_width)
    pre_act = jnp.einsum(
        "rgj,gjk->rgk", grouped, channel_blocks, preferred_element_type=jnp.float32
    )
    activated = jax.nn.gelu(pre_act).astype(jnp.bfloat16)
    every_activated = gather_groups(activated.reshape(rows_local, block_width))
    added = jnp.einsum("grk,kg->rk", every_activated.astype(jnp.float32), mix_out)
    outputs = (
        (grouped.astype(jnp.float32).reshape(rows_local, width_local) + added)
        .astype(jnp.bfloat16)
    )
    pre_grad = jax.vjp(jax.nn.gelu, pre_act)[1](act_grad.astype(jnp.float32))[0].astype(
        jnp.bfloat16
    )
    back_term = jnp.einsum(
        "rgk,gjk->rgj", pre_grad, channel_blocks, preferred_element_type=jnp.float32
    )
    hidden_grad = (upstream.astype(jnp.float32) + back_term).astype(jnp.bfloat16)
    channel_grad = jnp.transpose(
        lax.psum_scatter(
            jnp.einsum("rgj,rgk->jgk", grouped, pre_grad, preferred_element_type=jnp.float32),
            "seq",
            scatter_dimension=0,
            tiled=True,
        ),
        (1, 0, 2),
    )
    grad_cube = hidden_grad.astype(jnp.float32).reshape(count_a, length_q, width_local)
    gated_grad = (grad_cube * slope_out).astype(jnp.bfloat16)
    turned_grad = to_columns(gated_grad)
    second_grad = jnp.einsum(
        "cea,ecd->acd", second_blocks, turned_grad, preferred_element_type=jnp.float32
    ).astype(jnp.bfloat16)
    first_grad = to_rows(second_grad).reshape(count_a, length_q, width_local)
    block_grad = jnp.transpose(
        lax.psum_scatter(
            jnp.einsum("acd,abd->cab", first_grad, gated, preferred_element_type=jnp.float32),
            "ch",
            scatter_dimension=0,
            tiled=True,
        ),
        (1, 0, 2),
    )
    spread = jnp.einsum(
        "acb,acd->abd", first_blocks, first_grad, preferred_element_type=jnp.float32
    )
    input_grad = grad_cube + spread * (slope_in + gate_in * source * slope_in * (1.0 - slope_in))
    input_grad = input_grad + grad_cube * returned * slope_out * (1.0 - slope_out) * gate_out
    input_grad = input_grad.astype(jnp.bfloat16).reshape(rows_local, width_local)
    return (outputs, input_grad, channel_grad, block_grad)


def solution(mesh):
    placed = (
        P("seq", "ch"),
        P("ch"),
        P("ch"),
        P("seq", None, None),
        P("seq", None, None),
        P("ch", None, None),
        P(),
        P("seq", "ch"),
    )
    return jax.shard_map(
        on_device,
        mesh=mesh,
        in_specs=placed,
        out_specs=(P("seq", "ch"), P("seq", "ch"), P("ch", "seq", None), P("seq", "ch", None)),
        check_vma=False,
    )
```

```python
import jax
import jax.numpy as jnp
from jax import lax
from jax.sharding import PartitionSpec as P

F32 = jnp.float32
BF16 = jnp.bfloat16
RING_LIMIT = 16


def to_shift_order(x, me, n, axis=0):
    return jnp.take(x, (me + jnp.arange(n)) % n, axis=axis)


def to_source_order(x, me, n, axis=0):
    return jnp.take(x, (me - jnp.arange(n)) % n, axis=axis)


def exchange(pieces, axis_name):
    n = pieces.shape[0]
    if n > RING_LIMIT:
        me = lax.axis_index(axis_name)
        by_target = jnp.take(pieces, (jnp.arange(n) - me) % n, axis=0)
        arrived = lax.all_to_all(by_target, axis_name, 0, 0, tiled=True)
        return to_source_order(arrived, me, n)
    got = [pieces[0]]
    for k in range(1, n):
        got.append(lax.ppermute(pieces[k], axis_name, [(i, (i + k) % n) for i in range(n)]))
    return jnp.stack(got)


def split_rows(x, n):
    return x.reshape(n, x.shape[0] // n, *x.shape[1:])


def on_device(
    inputs, gate_in, gate_out, first_blocks, second_blocks, channel_blocks, group_mix, cotangent
):
    n = lax.axis_size("seq")
    m = lax.axis_size("ch")
    s_me = lax.axis_index("seq")
    g_me = lax.axis_index("ch")
    rows, width = inputs.shape
    length_q = first_blocks.shape[1]
    block_width = channel_blocks.shape[1]
    kq = block_width // m

    mix_f = group_mix.astype(F32)
    mix_mine = lax.dynamic_slice_in_dim(mix_f, g_me * kq, kq, 0)
    plus_m = (g_me + jnp.arange(m)) % m
    minus_m = (g_me - jnp.arange(m)) % m
    mix_fwd = jnp.take(jnp.take(mix_mine, minus_m, axis=1), plus_m, axis=2)
    mix_bwd = jnp.take(jnp.take(mix_mine, plus_m, axis=1), minus_m, axis=2)

    second_f = second_blocks.astype(F32)
    plus_n = (s_me + jnp.arange(n)) % n
    minus_n = (s_me - jnp.arange(n)) % n
    second_fwd = jnp.take(jnp.take(second_f, plus_n, axis=1), minus_n, axis=2)
    second_bwd = jnp.take(jnp.take(second_f, minus_n, axis=1), plus_n, axis=2)

    upstream = cotangent
    cot_pieces = to_shift_order(upstream.reshape(rows, m, kq), g_me, m, axis=1)
    cot_arrived = exchange(jnp.transpose(cot_pieces, (1, 0, 2)), "ch")
    act_grad_out = jnp.einsum(
        "krq,qpk->prq", cot_arrived.astype(F32), mix_bwd
    ).astype(BF16)
    act_grad_back = to_source_order(exchange(act_grad_out, "ch"), g_me, m)
    act_grad = jnp.transpose(act_grad_back, (1, 0, 2)).reshape(rows, block_width)

    source = inputs.astype(F32)
    slope_in = jax.nn.sigmoid(gate_in * source)
    gated = (source * slope_in).astype(BF16)
    mixed_first = jnp.dot(first_blocks[0], gated, preferred_element_type=F32).astype(BF16)
    first_arrived = exchange(to_shift_order(split_rows(mixed_first, n), s_me, n), "seq")
    second_out = jnp.einsum(
        "cpk,kcd->pcd", second_fwd, first_arrived.astype(F32)
    ).astype(BF16)
    second_back = to_source_order(exchange(second_out, "seq"), s_me, n)
    returned = second_back.reshape(rows, width).astype(F32)
    slope_out = jax.nn.sigmoid(gate_out * source)
    hidden = (source + returned * slope_out).astype(BF16)
    pre_act = jnp.dot(hidden, channel_blocks[0], preferred_element_type=F32)
    activated = jax.nn.gelu(pre_act).astype(BF16)

    act_pieces = to_shift_order(activated.reshape(rows, m, kq), g_me, m, axis=1)
    act_arrived = exchange(jnp.transpose(act_pieces, (1, 0, 2)), "ch")
    added_out = jnp.einsum("krq,qkp->prq", act_arrived.astype(F32), mix_fwd)
    added_back = to_source_order(exchange(added_out, "ch"), g_me, m)
    added = jnp.transpose(added_back, (1, 0, 2)).reshape(rows, block_width)
    outputs = (hidden.astype(F32) + added).astype(BF16)

    pre_grad = jax.vjp(jax.nn.gelu, pre_act)[1](act_grad.astype(F32))[0].astype(BF16)
    back_term = jnp.dot(pre_grad, channel_blocks[0].T, preferred_element_type=F32)
    hidden_grad = (upstream.astype(F32) + back_term).astype(BF16)
    channel_part = jnp.dot(hidden.T, pre_grad, preferred_element_type=F32)
    channel_arrived = exchange(to_shift_order(split_rows(channel_part, n), s_me, n), "seq")
    channel_grad = jnp.sum(channel_arrived, axis=0)[None]

    grad_flat = hidden_grad.astype(F32)
    gated_grad = (grad_flat * slope_out).astype(BF16)
    grad_arrived = exchange(to_shift_order(split_rows(gated_grad, n), s_me, n), "seq")
    first_out = jnp.einsum(
        "ckp,kcd->pcd", second_bwd, grad_arrived.astype(F32)
    ).astype(BF16)
    first_grad = to_source_order(exchange(first_out, "seq"), s_me, n).reshape(rows, width)
    block_part = jnp.dot(first_grad, gated.T, preferred_element_type=F32)
    block_arrived = exchange(to_shift_order(split_rows(block_part, m), g_me, m), "ch")
    block_grad = jnp.sum(block_arrived, axis=0)[None]

    spread = jnp.dot(first_blocks[0].T, first_grad, preferred_element_type=F32)
    input_grad = grad_flat + spread * (slope_in + gate_in * source * slope_in * (1.0 - slope_in))
    input_grad = input_grad + grad_flat * returned * slope_out * (1.0 - slope_out) * gate_out
    return (outputs, input_grad.astype(BF16), channel_grad, block_grad)


def solution(mesh):
    placed = (
        P("seq", "ch"),
        P("ch"),
        P("ch"),
        P("seq", None, None),
        P("seq", None, None),
        P("ch", None, None),
        P(),
        P("seq", "ch"),
    )
    return jax.shard_map(
        on_device,
        mesh=mesh,
        in_specs=placed,
        out_specs=(P("seq", "ch"), P("seq", "ch"), P("ch", "seq", None), P("seq", "ch", None)),
        check_vma=False,
    )
```

```python
import jax
import jax.numpy as jnp
from jax import lax
from jax.sharding import PartitionSpec as P

F32 = jnp.float32
BF16 = jnp.bfloat16
RING_LIMIT = 16


def to_shift_order(x, me, n, axis=0):
    return jnp.take(x, (me + jnp.arange(n)) % n, axis=axis)


def to_source_order(x, me, n, axis=0):
    return jnp.take(x, (me - jnp.arange(n)) % n, axis=axis)


def exchange(pieces, axis_name):
    n = pieces.shape[0]
    if n > RING_LIMIT:
        me = lax.axis_index(axis_name)
        by_target = jnp.take(pieces, (jnp.arange(n) - me) % n, axis=0)
        arrived = lax.all_to_all(by_target, axis_name, 0, 0, tiled=True)
        return to_source_order(arrived, me, n)
    got = [pieces[0]]
    for k in range(1, n):
        got.append(lax.ppermute(pieces[k], axis_name, [(i, (i + k) % n) for i in range(n)]))
    return jnp.stack(got)


def swap(pieces, axis_name):
    return lax.all_to_all(pieces, axis_name, 0, 0, tiled=True)


def split_rows(x, n):
    return x.reshape(n, x.shape[0] // n, *x.shape[1:])


def on_device(
    inputs, gate_in, gate_out, first_blocks, second_blocks, channel_blocks, group_mix, cotangent
):
    n = lax.axis_size("seq")
    m = lax.axis_size("ch")
    s_me = lax.axis_index("seq")
    g_me = lax.axis_index("ch")
    rows, width = inputs.shape
    length_q = first_blocks.shape[1]
    block_width = channel_blocks.shape[1]
    kq = block_width // m

    mix_f = group_mix.astype(F32)
    mix_mine = lax.dynamic_slice_in_dim(mix_f, g_me * kq, kq, 0)
    plus_m = (g_me + jnp.arange(m)) % m
    minus_m = (g_me - jnp.arange(m)) % m
    mix_fwd = jnp.take(jnp.take(mix_mine, minus_m, axis=1), plus_m, axis=2)
    mix_bwd = jnp.take(jnp.take(mix_mine, plus_m, axis=1), minus_m, axis=2)

    second_f = second_blocks.astype(F32)

    upstream = cotangent
    cot_pieces = to_shift_order(upstream.reshape(rows, m, kq), g_me, m, axis=1)
    cot_arrived = exchange(jnp.transpose(cot_pieces, (1, 0, 2)), "ch")
    act_grad_out = jnp.einsum(
        "krq,qpk->prq", cot_arrived.astype(F32), mix_bwd
    ).astype(BF16)
    act_grad_back = to_source_order(exchange(act_grad_out, "ch"), g_me, m)
    act_grad = jnp.transpose(act_grad_back, (1, 0, 2)).reshape(rows, block_width)

    source = inputs.astype(F32)
    slope_in = jax.nn.sigmoid(gate_in * source)
    gated = (source * slope_in).astype(BF16)
    mixed_first = jnp.dot(first_blocks[0], gated, preferred_element_type=F32).astype(BF16)
    first_arrived = swap(split_rows(mixed_first, n), "seq")
    second_out = jnp.einsum(
        "cea,acd->ecd", second_f, first_arrived.astype(F32)
    ).astype(BF16)
    returned = swap(second_out, "seq").reshape(rows, width).astype(F32)
    slope_out = jax.nn.sigmoid(gate_out * source)
    hidden = (source + returned * slope_out).astype(BF16)
    pre_act = jnp.dot(hidden, channel_blocks[0], preferred_element_type=F32)
    activated = jax.nn.gelu(pre_act).astype(BF16)

    act_pieces = to_shift_order(activated.reshape(rows, m, kq), g_me, m, axis=1)
    act_arrived = exchange(jnp.transpose(act_pieces, (1, 0, 2)), "ch")
    added_out = jnp.einsum("krq,qkp->prq", act_arrived.astype(F32), mix_fwd)
    added_back = to_source_order(exchange(added_out, "ch"), g_me, m)
    added = jnp.transpose(added_back, (1, 0, 2)).reshape(rows, block_width)
    outputs = (hidden.astype(F32) + added).astype(BF16)

    pre_grad = jax.vjp(jax.nn.gelu, pre_act)[1](act_grad.astype(F32))[0].astype(BF16)
    back_term = jnp.dot(pre_grad, channel_blocks[0].T, preferred_element_type=F32)
    hidden_grad = (upstream.astype(F32) + back_term).astype(BF16)
    channel_part = jnp.dot(hidden.T, pre_grad, preferred_element_type=F32)
    channel_arrived = swap(split_rows(channel_part, n), "seq")
    channel_grad = jnp.sum(channel_arrived, axis=0)[None]

    grad_flat = hidden_grad.astype(F32)
    gated_grad = (grad_flat * slope_out).astype(BF16)
    grad_arrived = swap(split_rows(gated_grad, n), "seq")
    first_out = jnp.einsum(
        "cea,ecd->acd", second_f, grad_arrived.astype(F32)
    ).astype(BF16)
    first_grad = swap(first_out, "seq").reshape(rows, width)
    block_part = jnp.dot(first_grad, gated.T, preferred_element_type=F32)
    block_arrived = exchange(to_shift_order(split_rows(block_part, m), g_me, m), "ch")
    block_grad = jnp.sum(block_arrived, axis=0)[None]

    spread = jnp.dot(first_blocks[0].T, first_grad, preferred_element_type=F32)
    input_grad = grad_flat + spread * (slope_in + gate_in * source * slope_in * (1.0 - slope_in))
    input_grad = input_grad + grad_flat * returned * slope_out * (1.0 - slope_out) * gate_out
    return (outputs, input_grad.astype(BF16), channel_grad, block_grad)


def solution(mesh):
    placed = (
        P("seq", "ch"),
        P("ch"),
        P("ch"),
        P("seq", None, None),
        P("seq", None, None),
        P("ch", None, None),
        P(),
        P("seq", "ch"),
    )
    return jax.shard_map(
        on_device,
        mesh=mesh,
        in_specs=placed,
        out_specs=(P("seq", "ch"), P("seq", "ch"), P("ch", "seq", None), P("seq", "ch", None)),
        check_vma=False,
    )
```

```python
import jax
import jax.numpy as jnp
from jax import lax
from jax.sharding import PartitionSpec as P

F32 = jnp.float32
BF16 = jnp.bfloat16
RING_LIMIT = 16


def to_shift_order(x, me, n, axis=0):
    return jnp.take(x, (me + jnp.arange(n)) % n, axis=axis)


def to_source_order(x, me, n, axis=0):
    return jnp.take(x, (me - jnp.arange(n)) % n, axis=axis)


def exchange(pieces, axis_name):
    n = pieces.shape[0]
    if n > RING_LIMIT:
        me = lax.axis_index(axis_name)
        by_target = jnp.take(pieces, (jnp.arange(n) - me) % n, axis=0)
        arrived = lax.all_to_all(by_target, axis_name, 0, 0, tiled=True)
        return to_source_order(arrived, me, n)
    got = [pieces[0]]
    for k in range(1, n):
        got.append(lax.ppermute(pieces[k], axis_name, [(i, (i + k) % n) for i in range(n)]))
    return jnp.stack(got)


def swap(pieces, axis_name):
    return lax.all_to_all(pieces, axis_name, 0, 0, tiled=True)


def split_rows(x, n):
    return x.reshape(n, x.shape[0] // n, *x.shape[1:])


def on_device(
    inputs, gate_in, gate_out, first_blocks, second_blocks, channel_blocks, group_mix, cotangent
):
    n = lax.axis_size("seq")
    m = lax.axis_size("ch")
    s_me = lax.axis_index("seq")
    g_me = lax.axis_index("ch")
    rows, width = inputs.shape
    length_q = first_blocks.shape[1]
    block_width = channel_blocks.shape[1]
    kq = block_width // m

    mix_f = group_mix.astype(F32)
    mix_mine = lax.dynamic_slice_in_dim(mix_f, g_me * kq, kq, 0)
    plus_m = (g_me + jnp.arange(m)) % m
    minus_m = (g_me - jnp.arange(m)) % m
    mix_fwd = jnp.take(jnp.take(mix_mine, minus_m, axis=1), plus_m, axis=2)
    mix_bwd = jnp.take(jnp.take(mix_mine, plus_m, axis=1), minus_m, axis=2)

    second_f = second_blocks.astype(F32)

    source = inputs.astype(F32)
    slope_in = jax.nn.sigmoid(gate_in * source)
    gated = (source * slope_in).astype(BF16)
    mixed_first = jnp.dot(first_blocks[0], gated, preferred_element_type=F32).astype(BF16)
    first_arrived = swap(split_rows(mixed_first, n), "seq")

    upstream = cotangent
    upstream_late, first_arrived = lax.optimization_barrier((upstream, first_arrived))
    cot_pieces = to_shift_order(upstream_late.reshape(rows, m, kq), g_me, m, axis=1)
    cot_arrived = exchange(jnp.transpose(cot_pieces, (1, 0, 2)), "ch")
    act_grad_out = jnp.einsum(
        "krq,qpk->prq", cot_arrived.astype(F32), mix_bwd
    ).astype(BF16)
    act_grad_back = to_source_order(exchange(act_grad_out, "ch"), g_me, m)
    act_grad = jnp.transpose(act_grad_back, (1, 0, 2)).reshape(rows, block_width)
    second_out = jnp.einsum(
        "cea,acd->ecd", second_f, first_arrived.astype(F32)
    ).astype(BF16)
    returned = swap(second_out, "seq").reshape(rows, width).astype(F32)
    slope_out = jax.nn.sigmoid(gate_out * source)
    hidden = (source + returned * slope_out).astype(BF16)
    pre_act = jnp.dot(hidden, channel_blocks[0], preferred_element_type=F32)
    activated = jax.nn.gelu(pre_act).astype(BF16)

    act_pieces = to_shift_order(activated.reshape(rows, m, kq), g_me, m, axis=1)
    act_arrived = exchange(jnp.transpose(act_pieces, (1, 0, 2)), "ch")
    added_out = jnp.einsum("krq,qkp->prq", act_arrived.astype(F32), mix_fwd).astype(BF16)
    added_back = to_source_order(exchange(added_out, "ch"), g_me, m)

    pre_grad = jax.vjp(jax.nn.gelu, pre_act)[1](act_grad.astype(F32))[0].astype(BF16)
    back_term = jnp.dot(pre_grad, channel_blocks[0].T, preferred_element_type=F32)
    hidden_grad = (upstream.astype(F32) + back_term).astype(BF16)
    channel_part = jnp.dot(hidden.T, pre_grad, preferred_element_type=F32)

    grad_flat = hidden_grad.astype(F32)
    gated_grad = (grad_flat * slope_out).astype(BF16)
    grad_arrived = swap(split_rows(gated_grad, n), "seq")
    first_out = jnp.einsum(
        "cea,ecd->acd", second_f, grad_arrived.astype(F32)
    ).astype(BF16)
    first_grad = swap(first_out, "seq").reshape(rows, width)
    first_grad, added_back, channel_part = lax.optimization_barrier(
        (first_grad, added_back, channel_part)
    )
    added = jnp.transpose(added_back, (1, 0, 2)).reshape(rows, block_width)
    outputs = (hidden.astype(F32) + added.astype(F32)).astype(BF16)
    block_part = jnp.dot(first_grad, gated.T, preferred_element_type=F32)
    block_arrived = exchange(to_shift_order(split_rows(block_part, m), g_me, m), "ch")
    block_grad = jnp.sum(block_arrived, axis=0)[None]
    channel_arrived = swap(split_rows(channel_part, n), "seq")
    channel_grad = jnp.sum(channel_arrived, axis=0)[None]

    spread = jnp.dot(first_blocks[0].T, first_grad, preferred_element_type=F32)
    input_grad = grad_flat + spread * (slope_in + gate_in * source * slope_in * (1.0 - slope_in))
    input_grad = input_grad + grad_flat * returned * slope_out * (1.0 - slope_out) * gate_out
    return (outputs, input_grad.astype(BF16), channel_grad, block_grad)


def solution(mesh):
    placed = (
        P("seq", "ch"),
        P("ch"),
        P("ch"),
        P("seq", None, None),
        P("seq", None, None),
        P("ch", None, None),
        P(),
        P("seq", "ch"),
    )
    return jax.shard_map(
        on_device,
        mesh=mesh,
        in_specs=placed,
        out_specs=(P("seq", "ch"), P("seq", "ch"), P("ch", "seq", None), P("seq", "ch", None)),
        check_vma=False,
    )
```

```python
import jax
import jax.numpy as jnp
from jax import lax
from jax.sharding import PartitionSpec as P

F32 = jnp.float32
BF16 = jnp.bfloat16
RING_LIMIT = 16


def to_shift_order(x, me, n, axis=0):
    return jnp.take(x, (me + jnp.arange(n)) % n, axis=axis)


def to_source_order(x, me, n, axis=0):
    return jnp.take(x, (me - jnp.arange(n)) % n, axis=axis)


def exchange(pieces, axis_name):
    n = pieces.shape[0]
    if n > RING_LIMIT:
        me = lax.axis_index(axis_name)
        by_target = jnp.take(pieces, (jnp.arange(n) - me) % n, axis=0)
        arrived = lax.all_to_all(by_target, axis_name, 0, 0, tiled=True)
        return to_source_order(arrived, me, n)
    got = [pieces[0]]
    for k in range(1, n):
        got.append(lax.ppermute(pieces[k], axis_name, [(i, (i + k) % n) for i in range(n)]))
    return jnp.stack(got)


def swap(pieces, axis_name):
    return lax.all_to_all(pieces, axis_name, 0, 0, tiled=True)


def split_rows(x, n):
    return x.reshape(n, x.shape[0] // n, *x.shape[1:])


def on_device(
    inputs, gate_in, gate_out, first_blocks, second_blocks, channel_blocks, group_mix, cotangent
):
    n = lax.axis_size("seq")
    m = lax.axis_size("ch")
    s_me = lax.axis_index("seq")
    g_me = lax.axis_index("ch")
    rows, width = inputs.shape
    length_q = first_blocks.shape[1]
    block_width = channel_blocks.shape[1]
    kq = block_width // m

    mix_f = group_mix.astype(F32)
    mix_mine = lax.dynamic_slice_in_dim(mix_f, g_me * kq, kq, 0)
    plus_m = (g_me + jnp.arange(m)) % m
    minus_m = (g_me - jnp.arange(m)) % m
    mix_fwd = jnp.take(jnp.take(mix_mine, minus_m, axis=1), plus_m, axis=2)
    mix_bwd = jnp.take(jnp.take(mix_mine, plus_m, axis=1), minus_m, axis=2)

    second_f = second_blocks.astype(F32)

    source = inputs.astype(F32)
    slope_in = jax.nn.sigmoid(gate_in * source)
    gated = (source * slope_in).astype(BF16)
    mixed_first = jnp.dot(first_blocks[0], gated, preferred_element_type=F32).astype(BF16)
    upstream = cotangent
    upstream_late, mixed_first = lax.optimization_barrier((upstream, mixed_first))
    first_arrived = swap(split_rows(mixed_first, n), "seq")
    cot_pieces = to_shift_order(upstream_late.reshape(rows, m, kq), g_me, m, axis=1)
    cot_arrived = exchange(jnp.transpose(cot_pieces, (1, 0, 2)), "ch")
    act_grad_out = jnp.einsum(
        "krq,qpk->prq", cot_arrived.astype(F32), mix_bwd
    ).astype(BF16)
    act_grad_back = to_source_order(exchange(act_grad_out, "ch"), g_me, m)
    act_grad = jnp.transpose(act_grad_back, (1, 0, 2)).reshape(rows, block_width)
    second_out = jnp.einsum(
        "cea,acd->ecd", second_f, first_arrived.astype(F32)
    ).astype(BF16)
    returned = swap(second_out, "seq").reshape(rows, width).astype(F32)
    slope_out = jax.nn.sigmoid(gate_out * source)
    hidden = (source + returned * slope_out).astype(BF16)
    pre_act = jnp.dot(hidden, channel_blocks[0], preferred_element_type=F32)
    activated = jax.nn.gelu(pre_act).astype(BF16)

    act_pieces = to_shift_order(activated.reshape(rows, m, kq), g_me, m, axis=1)
    act_arrived = exchange(jnp.transpose(act_pieces, (1, 0, 2)), "ch")
    added_out = jnp.einsum("krq,qkp->prq", act_arrived.astype(F32), mix_fwd).astype(BF16)
    added_back = to_source_order(exchange(added_out, "ch"), g_me, m)

    pre_grad = jax.vjp(jax.nn.gelu, pre_act)[1](act_grad.astype(F32))[0].astype(BF16)
    back_term = jnp.dot(pre_grad, channel_blocks[0].T, preferred_element_type=F32)
    hidden_grad = (upstream.astype(F32) + back_term).astype(BF16)
    channel_part = jnp.dot(hidden.T, pre_grad, preferred_element_type=F32)

    grad_flat = hidden_grad.astype(F32)
    gated_grad = (grad_flat * slope_out).astype(BF16)
    grad_arrived = swap(split_rows(gated_grad, n), "seq")
    first_out = jnp.einsum(
        "cea,ecd->acd", second_f, grad_arrived.astype(F32)
    ).astype(BF16)
    first_grad = swap(first_out, "seq").reshape(rows, width)
    first_grad, added_back, channel_part = lax.optimization_barrier(
        (first_grad, added_back, channel_part)
    )
    added = jnp.transpose(added_back, (1, 0, 2)).reshape(rows, block_width)
    outputs = (hidden.astype(F32) + added.astype(F32)).astype(BF16)
    block_part = jnp.dot(first_grad, gated.T, preferred_element_type=F32)
    block_pieces = to_shift_order(split_rows(block_part, m), g_me, m).astype(BF16)
    block_grad = jnp.sum(exchange(block_pieces, "ch").astype(F32), axis=0)[None]
    channel_arrived = swap(split_rows(channel_part, n).astype(BF16), "seq")
    channel_grad = jnp.sum(channel_arrived.astype(F32), axis=0)[None]

    spread = jnp.dot(first_blocks[0].T, first_grad, preferred_element_type=F32)
    input_grad = grad_flat + spread * (slope_in + gate_in * source * slope_in * (1.0 - slope_in))
    input_grad = input_grad + grad_flat * returned * slope_out * (1.0 - slope_out) * gate_out
    return (outputs, input_grad.astype(BF16), channel_grad, block_grad)


def solution(mesh):
    placed = (
        P("seq", "ch"),
        P("ch"),
        P("ch"),
        P("seq", None, None),
        P("seq", None, None),
        P("ch", None, None),
        P(),
        P("seq", "ch"),
    )
    return jax.shard_map(
        on_device,
        mesh=mesh,
        in_specs=placed,
        out_specs=(P("seq", "ch"), P("seq", "ch"), P("ch", "seq", None), P("seq", "ch", None)),
        check_vma=False,
    )
```

```python
import jax
import jax.numpy as jnp
from jax import lax
from jax.sharding import PartitionSpec as P

F32 = jnp.float32
BF16 = jnp.bfloat16


def exchange(pieces, axis_name):
    n = len(pieces)
    got = [pieces[0]]
    for k in range(1, n):
        got.append(lax.ppermute(pieces[k], axis_name, [(i, (i + k) % n) for i in range(n)]))
    return got


def swap(pieces, axis_name):
    return lax.all_to_all(pieces, axis_name, 0, 0, tiled=True)


def split_rows(x, n):
    return x.reshape(n, x.shape[0] // n, *x.shape[1:])


def lane_chunk(x, index, size):
    return lax.dynamic_slice_in_dim(x, index * size, size, axis=1)


def place_chunks(chunks, starts, like):
    out = jnp.zeros(like.shape, like.dtype)
    for chunk, start in zip(chunks, starts):
        out = lax.dynamic_update_slice_in_dim(out, chunk, start, axis=1)
    return out


def on_device(
    inputs, gate_in, gate_out, first_blocks, second_blocks, channel_blocks, group_mix, cotangent
):
    n = lax.axis_size("seq")
    m = lax.axis_size("ch")
    g_me = lax.axis_index("ch")
    rows, width = inputs.shape
    block_width = channel_blocks.shape[1]
    kq = block_width // m
    chunk_of = [(g_me + k) % m for k in range(m)]
    origin_of = [(g_me - k) % m for k in range(m)]

    mix_mine = lax.dynamic_slice_in_dim(group_mix, g_me * kq, kq, 0).astype(F32)

    def coefficient(g, h):
        return lax.dynamic_slice(mix_mine, (0, g, h), (kq, 1, 1)).reshape(1, kq)

    second_f = second_blocks.astype(F32)

    source = inputs.astype(F32)
    slope_in = jax.nn.sigmoid(gate_in * source)
    gated = (source * slope_in).astype(BF16)
    mixed_first = jnp.dot(first_blocks[0], gated, preferred_element_type=F32).astype(BF16)

    upstream = cotangent
    upstream_late, mixed_first = lax.optimization_barrier((upstream, mixed_first))
    cot_arrived = exchange([lane_chunk(upstream_late, t, kq) for t in chunk_of], "ch")
    act_grad_out = [
        sum(
            cot_arrived[k].astype(F32) * coefficient(chunk_of[p], origin_of[k])
            for k in range(m)
        ).astype(BF16)
        for p in range(m)
    ]
    act_grad_back = exchange(act_grad_out, "ch")
    act_grad = place_chunks(act_grad_back, [t * kq for t in origin_of], upstream)

    first_arrived = swap(split_rows(mixed_first, n), "seq")
    second_out = jnp.einsum(
        "cea,acd->ecd", second_f, first_arrived.astype(F32)
    ).astype(BF16)
    returned = swap(second_out, "seq").reshape(rows, width).astype(F32)
    slope_out = jax.nn.sigmoid(gate_out * source)
    hidden = (source + returned * slope_out).astype(BF16)
    pre_act = jnp.dot(hidden, channel_blocks[0], preferred_element_type=F32)
    activated = jax.nn.gelu(pre_act).astype(BF16)

    act_arrived = exchange([lane_chunk(activated, t, kq) for t in chunk_of], "ch")
    added_out = [
        sum(
            act_arrived[k].astype(F32) * coefficient(origin_of[k], chunk_of[p])
            for k in range(m)
        ).astype(BF16)
        for p in range(m)
    ]
    added_back = exchange(added_out, "ch")

    pre_grad = jax.vjp(jax.nn.gelu, pre_act)[1](act_grad.astype(F32))[0].astype(BF16)
    back_term = jnp.dot(pre_grad, channel_blocks[0].T, preferred_element_type=F32)
    hidden_grad = (upstream.astype(F32) + back_term).astype(BF16)
    channel_part = jnp.dot(hidden.T, pre_grad, preferred_element_type=F32)

    grad_flat = hidden_grad.astype(F32)
    gated_grad = (grad_flat * slope_out).astype(BF16)
    grad_arrived = swap(split_rows(gated_grad, n), "seq")
    first_out = jnp.einsum(
        "cea,ecd->acd", second_f, grad_arrived.astype(F32)
    ).astype(BF16)
    first_grad = swap(first_out, "seq").reshape(rows, width)
    first_grad, added_back, channel_part = lax.optimization_barrier(
        (first_grad, added_back, channel_part)
    )
    outputs = place_chunks(
        [
            (lane_chunk(hidden, t, kq).astype(F32) + part.astype(F32)).astype(BF16)
            for t, part in zip(origin_of, added_back)
        ],
        [t * kq for t in origin_of],
        hidden,
    )
    block_part = jnp.dot(first_grad, gated.T, preferred_element_type=F32)
    cq = block_part.shape[0] // m
    block_arrived = exchange(
        [lax.dynamic_slice_in_dim(block_part, t * cq, cq, 0).astype(BF16) for t in chunk_of],
        "ch",
    )
    block_grad = sum(part.astype(F32) for part in block_arrived)[None]
    channel_arrived = swap(split_rows(channel_part, n).astype(BF16), "seq")
    channel_grad = jnp.sum(channel_arrived.astype(F32), axis=0)[None]

    spread = jnp.dot(first_blocks[0].T, first_grad, preferred_element_type=F32)
    input_grad = grad_flat + spread * (slope_in + gate_in * source * slope_in * (1.0 - slope_in))
    input_grad = input_grad + grad_flat * returned * slope_out * (1.0 - slope_out) * gate_out
    return (outputs, input_grad.astype(BF16), channel_grad, block_grad)


def solution(mesh):
    placed = (
        P("seq", "ch"),
        P("ch"),
        P("ch"),
        P("seq", None, None),
        P("seq", None, None),
        P("ch", None, None),
        P(),
        P("seq", "ch"),
    )
    return jax.shard_map(
        on_device,
        mesh=mesh,
        in_specs=placed,
        out_specs=(P("seq", "ch"), P("seq", "ch"), P("ch", "seq", None), P("seq", "ch", None)),
        check_vma=False,
    )
```

```python
import jax
import jax.numpy as jnp
from jax import lax
from jax.sharding import PartitionSpec as P

F32 = jnp.float32
BF16 = jnp.bfloat16


def exchange(pieces, axis_name):
    n = len(pieces)
    got = [pieces[0]]
    for k in range(1, n):
        got.append(lax.ppermute(pieces[k], axis_name, [(i, (i + k) % n) for i in range(n)]))
    return got


def swap(pieces, axis_name):
    return lax.all_to_all(pieces, axis_name, 0, 0, tiled=True)


def split_rows(x, n):
    return x.reshape(n, x.shape[0] // n, *x.shape[1:])


def lane_chunk(x, index, size):
    return lax.dynamic_slice_in_dim(x, index * size, size, axis=1)


def place_chunks(chunks, starts, like):
    out = jnp.zeros(like.shape, like.dtype)
    for chunk, start in zip(chunks, starts):
        out = lax.dynamic_update_slice_in_dim(out, chunk, start, axis=1)
    return out


def on_device(
    inputs, gate_in, gate_out, first_blocks, second_blocks, channel_blocks, group_mix, cotangent
):
    n = lax.axis_size("seq")
    m = lax.axis_size("ch")
    g_me = lax.axis_index("ch")
    rows, width = inputs.shape
    block_width = channel_blocks.shape[1]
    kq = block_width // m
    chunk_of = [(g_me + k) % m for k in range(m)]
    origin_of = [(g_me - k) % m for k in range(m)]

    mix_mine = lax.dynamic_slice_in_dim(group_mix, g_me * kq, kq, 0).astype(F32)

    def coefficient(g, h):
        return lax.dynamic_slice(mix_mine, (0, g, h), (kq, 1, 1)).reshape(1, kq)

    second_f = second_blocks.astype(F32)

    source = inputs.astype(F32)
    slope_in = jax.nn.sigmoid(gate_in * source)
    gated = (source * slope_in).astype(BF16)
    mixed_first = jnp.dot(first_blocks[0], gated, preferred_element_type=F32).astype(BF16)

    upstream = cotangent
    upstream_late, mixed_first = lax.optimization_barrier((upstream, mixed_first))
    cot_arrived = exchange([lane_chunk(upstream_late, t, kq) for t in chunk_of], "ch")
    act_grad_out = [
        sum(
            cot_arrived[k].astype(F32) * coefficient(chunk_of[p], origin_of[k])
            for k in range(m)
        ).astype(BF16)
        for p in range(m)
    ]
    act_grad_back = exchange(act_grad_out, "ch")
    act_grad = place_chunks(act_grad_back, [t * kq for t in origin_of], upstream)

    first_arrived = swap(split_rows(mixed_first, n), "seq")
    second_out = jnp.einsum(
        "cea,acd->ecd", second_f, first_arrived.astype(F32)
    ).astype(BF16)
    returned = swap(second_out, "seq").reshape(rows, width).astype(F32)
    slope_out = jax.nn.sigmoid(gate_out * source)
    hidden = (source + returned * slope_out).astype(BF16)
    pre_act = jnp.dot(hidden, channel_blocks[0], preferred_element_type=F32)
    activated = jax.nn.gelu(pre_act).astype(BF16)

    act_arrived = exchange([lane_chunk(activated, t, kq) for t in chunk_of], "ch")
    added_out = [
        sum(
            act_arrived[k].astype(F32) * coefficient(origin_of[k], chunk_of[p])
            for k in range(m)
        ).astype(BF16)
        for p in range(m)
    ]
    added_back = exchange(added_out, "ch")

    pre_grad = jax.vjp(jax.nn.gelu, pre_act)[1](act_grad.astype(F32))[0].astype(BF16)
    back_term = jnp.dot(pre_grad, channel_blocks[0].T, preferred_element_type=F32)
    hidden_grad = (upstream.astype(F32) + back_term).astype(BF16)
    channel_part = jnp.dot(hidden.T, pre_grad, preferred_element_type=F32)

    grad_flat = hidden_grad.astype(F32)
    gated_grad = (grad_flat * slope_out).astype(BF16)
    grad_arrived = swap(split_rows(gated_grad, n), "seq")
    first_out = jnp.einsum(
        "cea,ecd->acd", second_f, grad_arrived.astype(F32)
    ).astype(BF16)
    first_grad = swap(first_out, "seq").reshape(rows, width)
    first_grad, channel_part = lax.optimization_barrier((first_grad, channel_part))
    block_part = jnp.dot(first_grad, gated.T, preferred_element_type=F32)
    block_part, added_back = lax.optimization_barrier((block_part, added_back))
    outputs = place_chunks(
        [
            (lane_chunk(hidden, t, kq).astype(F32) + part.astype(F32)).astype(BF16)
            for t, part in zip(origin_of, added_back)
        ],
        [t * kq for t in origin_of],
        hidden,
    )
    cq = block_part.shape[0] // m
    block_arrived = exchange(
        [lax.dynamic_slice_in_dim(block_part, t * cq, cq, 0).astype(BF16) for t in chunk_of],
        "ch",
    )
    block_grad = sum(part.astype(F32) for part in block_arrived)[None]
    channel_arrived = swap(split_rows(channel_part, n).astype(BF16), "seq")
    channel_grad = jnp.sum(channel_arrived.astype(F32), axis=0)[None]

    spread = jnp.dot(first_blocks[0].T, first_grad, preferred_element_type=F32)
    input_grad = grad_flat + spread * (slope_in + gate_in * source * slope_in * (1.0 - slope_in))
    input_grad = input_grad + grad_flat * returned * slope_out * (1.0 - slope_out) * gate_out
    return (outputs, input_grad.astype(BF16), channel_grad, block_grad)


def solution(mesh):
    placed = (
        P("seq", "ch"),
        P("ch"),
        P("ch"),
        P("seq", None, None),
        P("seq", None, None),
        P("ch", None, None),
        P(),
        P("seq", "ch"),
    )
    return jax.shard_map(
        on_device,
        mesh=mesh,
        in_specs=placed,
        out_specs=(P("seq", "ch"), P("seq", "ch"), P("ch", "seq", None), P("seq", "ch", None)),
        check_vma=False,
    )
```

```python
import jax
import jax.numpy as jnp
from jax import lax
from jax.sharding import PartitionSpec as P

F32 = jnp.float32
BF16 = jnp.bfloat16


def exchange(pieces, axis_name):
    n = len(pieces)
    got = [pieces[0]]
    for k in range(1, n):
        got.append(lax.ppermute(pieces[k], axis_name, [(i, (i + k) % n) for i in range(n)]))
    return got


def swap(pieces, axis_name):
    return lax.all_to_all(pieces, axis_name, 0, 0, tiled=True)


def split_rows(x, n):
    return x.reshape(n, x.shape[0] // n, *x.shape[1:])


def lane_chunk(x, index, size):
    return lax.dynamic_slice_in_dim(x, index * size, size, axis=1)


def place_chunks(chunks, starts, like):
    out = jnp.zeros(like.shape, like.dtype)
    for chunk, start in zip(chunks, starts):
        out = lax.dynamic_update_slice_in_dim(out, chunk, start, axis=1)
    return out


def on_device(
    inputs, gate_in, gate_out, first_blocks, second_blocks, channel_blocks, group_mix, cotangent
):
    n = lax.axis_size("seq")
    m = lax.axis_size("ch")
    g_me = lax.axis_index("ch")
    rows, width = inputs.shape
    block_width = channel_blocks.shape[1]
    kq = block_width // m
    chunk_of = [(g_me + k) % m for k in range(m)]
    origin_of = [(g_me - k) % m for k in range(m)]

    mix_mine = lax.dynamic_slice_in_dim(group_mix, g_me * kq, kq, 0).astype(F32)

    def coefficient(g, h):
        return lax.dynamic_slice(mix_mine, (0, g, h), (kq, 1, 1)).reshape(1, kq)

    second_f = second_blocks.astype(F32)

    source = inputs.astype(F32)
    slope_in = jax.nn.sigmoid(gate_in * source)
    gated = (source * slope_in).astype(BF16)
    mixed_first = jnp.dot(first_blocks[0], gated, preferred_element_type=F32).astype(BF16)

    upstream = cotangent
    upstream_late, mixed_first = lax.optimization_barrier((upstream, mixed_first))
    cot_arrived = exchange([lane_chunk(upstream_late, t, kq) for t in chunk_of], "ch")
    act_grad_out = [
        sum(
            cot_arrived[k].astype(F32) * coefficient(chunk_of[p], origin_of[k])
            for k in range(m)
        ).astype(BF16)
        for p in range(m)
    ]
    act_grad_back = exchange(act_grad_out, "ch")
    act_grad = place_chunks(act_grad_back, [t * kq for t in origin_of], upstream)

    first_arrived = swap(split_rows(mixed_first, n), "seq")
    second_out = jnp.einsum(
        "cea,acd->ecd", second_f, first_arrived.astype(F32)
    ).astype(BF16)
    returned = swap(second_out, "seq").reshape(rows, width).astype(F32)
    slope_out = jax.nn.sigmoid(gate_out * source)
    hidden = (source + returned * slope_out).astype(BF16)
    pre_act = jnp.dot(hidden, channel_blocks[0], preferred_element_type=F32)
    activated = jax.nn.gelu(pre_act).astype(BF16)

    act_arrived = exchange([lane_chunk(activated, t, kq) for t in chunk_of], "ch")
    added_out = [
        sum(
            act_arrived[k].astype(F32) * coefficient(origin_of[k], chunk_of[p])
            for k in range(m)
        ).astype(BF16)
        for p in range(m)
    ]
    added_back = exchange(added_out, "ch")

    pre_grad = jax.vjp(jax.nn.gelu, pre_act)[1](act_grad.astype(F32))[0].astype(BF16)
    back_term = jnp.dot(pre_grad, channel_blocks[0].T, preferred_element_type=F32)
    hidden_grad = (upstream.astype(F32) + back_term).astype(BF16)
    channel_part = jnp.dot(hidden.T, pre_grad, preferred_element_type=F32)

    grad_flat = hidden_grad.astype(F32)
    gated_grad = (grad_flat * slope_out).astype(BF16)
    grad_arrived = swap(split_rows(gated_grad, n), "seq")
    first_out = jnp.einsum(
        "cea,ecd->acd", second_f, grad_arrived.astype(F32)
    ).astype(BF16)
    first_grad = swap(first_out, "seq").reshape(rows, width)
    first_grad, channel_part = lax.optimization_barrier((first_grad, channel_part))
    block_part = jnp.dot(first_grad, gated.T, preferred_element_type=F32)
    cq = block_part.shape[0] // m
    block_arrived = exchange(
        [lax.dynamic_slice_in_dim(block_part, t * cq, cq, 0).astype(BF16) for t in chunk_of],
        "ch",
    )
    block_arrived, added_back = lax.optimization_barrier((block_arrived, added_back))
    block_grad = sum(part.astype(F32) for part in block_arrived)[None]
    outputs = place_chunks(
        [
            (lane_chunk(hidden, t, kq).astype(F32) + part.astype(F32)).astype(BF16)
            for t, part in zip(origin_of, added_back)
        ],
        [t * kq for t in origin_of],
        hidden,
    )
    channel_arrived = swap(split_rows(channel_part, n).astype(BF16), "seq")
    channel_grad = jnp.sum(channel_arrived.astype(F32), axis=0)[None]

    spread = jnp.dot(first_blocks[0].T, first_grad, preferred_element_type=F32)
    input_grad = grad_flat + spread * (slope_in + gate_in * source * slope_in * (1.0 - slope_in))
    input_grad = input_grad + grad_flat * returned * slope_out * (1.0 - slope_out) * gate_out
    return (outputs, input_grad.astype(BF16), channel_grad, block_grad)


def solution(mesh):
    placed = (
        P("seq", "ch"),
        P("ch"),
        P("ch"),
        P("seq", None, None),
        P("seq", None, None),
        P("ch", None, None),
        P(),
        P("seq", "ch"),
    )
    return jax.shard_map(
        on_device,
        mesh=mesh,
        in_specs=placed,
        out_specs=(P("seq", "ch"), P("seq", "ch"), P("ch", "seq", None), P("seq", "ch", None)),
        check_vma=False,
    )
```

```python
import jax
import jax.numpy as jnp
from jax import lax
from jax.sharding import PartitionSpec as P

F32 = jnp.float32
BF16 = jnp.bfloat16


def exchange(pieces, axis_name):
    n = len(pieces)
    got = [pieces[0]]
    for k in range(1, n):
        got.append(lax.ppermute(pieces[k], axis_name, [(i, (i + k) % n) for i in range(n)]))
    return got


def swap(pieces, axis_name):
    return lax.all_to_all(pieces, axis_name, 0, 0, tiled=True)


def split_rows(x, n):
    return x.reshape(n, x.shape[0] // n, *x.shape[1:])


def lane_chunk(x, index, size):
    return lax.dynamic_slice_in_dim(x, index * size, size, axis=1)


def place_chunks(chunks, starts, like):
    out = jnp.zeros(like.shape, like.dtype)
    for chunk, start in zip(chunks, starts):
        out = lax.dynamic_update_slice_in_dim(out, chunk, start, axis=1)
    return out


def on_device(
    inputs, gate_in, gate_out, first_blocks, second_blocks, channel_blocks, group_mix, cotangent
):
    n = lax.axis_size("seq")
    m = lax.axis_size("ch")
    g_me = lax.axis_index("ch")
    rows, width = inputs.shape
    block_width = channel_blocks.shape[1]
    kq = block_width // m
    chunk_of = [(g_me + k) % m for k in range(m)]
    origin_of = [(g_me - k) % m for k in range(m)]

    mix_mine = lax.dynamic_slice_in_dim(group_mix, g_me * kq, kq, 0).astype(F32)

    def coefficient(g, h):
        return lax.dynamic_slice(mix_mine, (0, g, h), (kq, 1, 1)).reshape(1, kq)

    second_f = second_blocks.astype(F32)

    source = inputs.astype(F32)
    slope_in = jax.nn.sigmoid(gate_in * source)
    gated = (source * slope_in).astype(BF16)
    mixed_first = jnp.dot(first_blocks[0], gated, preferred_element_type=F32).astype(BF16)

    upstream = cotangent
    upstream_late, mixed_first = lax.optimization_barrier((upstream, mixed_first))
    cot_arrived = exchange([lane_chunk(upstream_late, t, kq) for t in chunk_of], "ch")
    act_grad_out = [
        sum(
            cot_arrived[k].astype(F32) * coefficient(chunk_of[p], origin_of[k])
            for k in range(m)
        ).astype(BF16)
        for p in range(m)
    ]
    act_grad_back = exchange(act_grad_out, "ch")
    act_grad = place_chunks(act_grad_back, [t * kq for t in origin_of], upstream)

    first_arrived = swap(split_rows(mixed_first, n), "seq")
    second_out = jnp.einsum(
        "cea,acd->ecd", second_f, first_arrived.astype(F32)
    ).astype(BF16)
    returned = swap(second_out, "seq").reshape(rows, width).astype(F32)
    slope_out = jax.nn.sigmoid(gate_out * source)
    hidden = (source + returned * slope_out).astype(BF16)
    pre_act = jnp.dot(hidden, channel_blocks[0], preferred_element_type=F32)
    activated = jax.nn.gelu(pre_act).astype(BF16)

    act_arrived = exchange([lane_chunk(activated, t, kq) for t in chunk_of], "ch")
    added_out = [
        sum(
            act_arrived[k].astype(F32) * coefficient(origin_of[k], chunk_of[p])
            for k in range(m)
        ).astype(BF16)
        for p in range(m)
    ]
    added_back = exchange(added_out, "ch")

    pre_grad = jax.vjp(jax.nn.gelu, pre_act)[1](act_grad.astype(F32))[0].astype(BF16)
    back_term = jnp.dot(pre_grad, channel_blocks[0].T, preferred_element_type=F32)
    hidden_grad = (upstream.astype(F32) + back_term).astype(BF16)
    channel_part = jnp.dot(hidden.T, pre_grad, preferred_element_type=F32)

    grad_flat = hidden_grad.astype(F32)
    gated_grad = (grad_flat * slope_out).astype(BF16)
    grad_arrived = swap(split_rows(gated_grad, n), "seq")
    first_out = jnp.einsum(
        "cea,ecd->acd", second_f, grad_arrived.astype(F32)
    ).astype(BF16)
    first_grad = swap(first_out, "seq").reshape(rows, width)
    first_grad, channel_part = lax.optimization_barrier((first_grad, channel_part))
    block_part = jnp.dot(first_grad, gated.T, preferred_element_type=F32)
    cq = block_part.shape[0] // m
    block_arrived = exchange(
        [lax.dynamic_slice_in_dim(block_part, t * cq, cq, 0).astype(BF16) for t in chunk_of],
        "ch",
    )
    first_block, added_back = lax.optimization_barrier((block_arrived[1], added_back))
    block_arrived[1] = first_block
    block_grad = sum(part.astype(F32) for part in block_arrived)[None]
    outputs = place_chunks(
        [
            (lane_chunk(hidden, t, kq).astype(F32) + part.astype(F32)).astype(BF16)
            for t, part in zip(origin_of, added_back)
        ],
        [t * kq for t in origin_of],
        hidden,
    )
    channel_arrived = swap(split_rows(channel_part, n).astype(BF16), "seq")
    channel_grad = jnp.sum(channel_arrived.astype(F32), axis=0)[None]

    spread = jnp.dot(first_blocks[0].T, first_grad, preferred_element_type=F32)
    input_grad = grad_flat + spread * (slope_in + gate_in * source * slope_in * (1.0 - slope_in))
    input_grad = input_grad + grad_flat * returned * slope_out * (1.0 - slope_out) * gate_out
    return (outputs, input_grad.astype(BF16), channel_grad, block_grad)


def solution(mesh):
    placed = (
        P("seq", "ch"),
        P("ch"),
        P("ch"),
        P("seq", None, None),
        P("seq", None, None),
        P("ch", None, None),
        P(),
        P("seq", "ch"),
    )
    return jax.shard_map(
        on_device,
        mesh=mesh,
        in_specs=placed,
        out_specs=(P("seq", "ch"), P("seq", "ch"), P("ch", "seq", None), P("seq", "ch", None)),
        check_vma=False,
    )
```

```python
import jax
import jax.numpy as jnp
from jax import lax
from jax.sharding import PartitionSpec as P

F32 = jnp.float32
BF16 = jnp.bfloat16


def exchange(pieces, axis_name):
    n = len(pieces)
    got = [pieces[0]]
    for k in range(1, n):
        got.append(lax.ppermute(pieces[k], axis_name, [(i, (i + k) % n) for i in range(n)]))
    return got


def swap(pieces, axis_name):
    return lax.all_to_all(pieces, axis_name, 0, 0, tiled=True)


def split_rows(x, n):
    return x.reshape(n, x.shape[0] // n, *x.shape[1:])


def lane_chunk(x, index, size):
    return lax.dynamic_slice_in_dim(x, index * size, size, axis=1)


def place_chunks(chunks, starts, like):
    out = jnp.zeros(like.shape, like.dtype)
    for chunk, start in zip(chunks, starts):
        out = lax.dynamic_update_slice_in_dim(out, chunk, start, axis=1)
    return out


def on_device(
    inputs, gate_in, gate_out, first_blocks, second_blocks, channel_blocks, group_mix, cotangent
):
    n = lax.axis_size("seq")
    m = lax.axis_size("ch")
    g_me = lax.axis_index("ch")
    rows, width = inputs.shape
    block_width = channel_blocks.shape[1]
    kq = block_width // m
    chunk_of = [(g_me + k) % m for k in range(m)]
    origin_of = [(g_me - k) % m for k in range(m)]

    mix_mine = lax.dynamic_slice_in_dim(group_mix, g_me * kq, kq, 0).astype(F32)

    def coefficient(g, h):
        return lax.dynamic_slice(mix_mine, (0, g, h), (kq, 1, 1)).reshape(1, kq)

    second_f = second_blocks.astype(F32)

    source = inputs.astype(F32)
    slope_in = jax.nn.sigmoid(gate_in * source)
    gated = (source * slope_in).astype(BF16)
    mixed_first = jnp.dot(first_blocks[0], gated, preferred_element_type=F32).astype(BF16)

    upstream = cotangent
    upstream_late, mixed_first = lax.optimization_barrier((upstream, mixed_first))
    cot_arrived = exchange([lane_chunk(upstream_late, t, kq) for t in chunk_of], "ch")
    act_grad_out = [
        sum(
            cot_arrived[k].astype(F32) * coefficient(chunk_of[p], origin_of[k])
            for k in range(m)
        ).astype(BF16)
        for p in range(m)
    ]
    act_grad_back = exchange(act_grad_out, "ch")
    act_grad = place_chunks(act_grad_back, [t * kq for t in origin_of], upstream)

    first_arrived = swap(split_rows(mixed_first, n), "seq")
    second_out = jnp.einsum(
        "cea,acd->ecd", second_f, first_arrived.astype(F32)
    ).astype(BF16)
    returned = swap(second_out, "seq").reshape(rows, width).astype(F32)
    slope_out = jax.nn.sigmoid(gate_out * source)
    hidden = (source + returned * slope_out).astype(BF16)
    pre_act = jnp.dot(hidden, channel_blocks[0], preferred_element_type=F32)
    activated = jax.nn.gelu(pre_act).astype(BF16)

    act_arrived = exchange([lane_chunk(activated, t, kq) for t in chunk_of], "ch")
    added_out = [
        sum(
            act_arrived[k].astype(F32) * coefficient(origin_of[k], chunk_of[p])
            for k in range(m)
        ).astype(BF16)
        for p in range(m)
    ]
    added_back = exchange(added_out, "ch")

    pre_grad = jax.vjp(jax.nn.gelu, pre_act)[1](act_grad.astype(F32))[0].astype(BF16)
    back_term = jnp.dot(pre_grad, channel_blocks[0].T, preferred_element_type=F32)
    hidden_grad = (upstream.astype(F32) + back_term).astype(BF16)
    channel_part = jnp.dot(hidden.T, pre_grad, preferred_element_type=F32)

    grad_flat = hidden_grad.astype(F32)
    gated_grad = (grad_flat * slope_out).astype(BF16)
    grad_arrived = swap(split_rows(gated_grad, n), "seq")
    first_out = jnp.einsum(
        "cea,ecd->acd", second_f, grad_arrived.astype(F32)
    ).astype(BF16)
    first_grad = swap(first_out, "seq").reshape(rows, width)
    first_grad, channel_part = lax.optimization_barrier((first_grad, channel_part))
    block_part = jnp.dot(first_grad, gated.T, preferred_element_type=F32)
    cq = block_part.shape[0] // m
    block_arrived = exchange(
        [lax.dynamic_slice_in_dim(block_part, t * cq, cq, 0).astype(BF16) for t in chunk_of],
        "ch",
    )
    first_block, added_back, first_grad = lax.optimization_barrier(
        (block_arrived[1], added_back, first_grad)
    )
    block_arrived[1] = first_block
    block_grad = sum(part.astype(F32) for part in block_arrived)[None]
    outputs = place_chunks(
        [
            (lane_chunk(hidden, t, kq).astype(F32) + part.astype(F32)).astype(BF16)
            for t, part in zip(origin_of, added_back)
        ],
        [t * kq for t in origin_of],
        hidden,
    )
    channel_arrived = swap(split_rows(channel_part, n).astype(BF16), "seq")
    channel_grad = jnp.sum(channel_arrived.astype(F32), axis=0)[None]

    spread = jnp.dot(first_blocks[0].T, first_grad, preferred_element_type=F32)
    input_grad = grad_flat + spread * (slope_in + gate_in * source * slope_in * (1.0 - slope_in))
    input_grad = input_grad + grad_flat * returned * slope_out * (1.0 - slope_out) * gate_out
    return (outputs, input_grad.astype(BF16), channel_grad, block_grad)


def solution(mesh):
    placed = (
        P("seq", "ch"),
        P("ch"),
        P("ch"),
        P("seq", None, None),
        P("seq", None, None),
        P("ch", None, None),
        P(),
        P("seq", "ch"),
    )
    return jax.shard_map(
        on_device,
        mesh=mesh,
        in_specs=placed,
        out_specs=(P("seq", "ch"), P("seq", "ch"), P("ch", "seq", None), P("seq", "ch", None)),
        check_vma=False,
    )
```

```python
import jax
import jax.numpy as jnp
from jax import lax
from jax.sharding import PartitionSpec as P

F32 = jnp.float32
BF16 = jnp.bfloat16


def exchange(pieces, axis_name):
    n = len(pieces)
    got = [pieces[0]]
    for k in range(1, n):
        got.append(lax.ppermute(pieces[k], axis_name, [(i, (i + k) % n) for i in range(n)]))
    return got


def swap(pieces, axis_name):
    return lax.all_to_all(pieces, axis_name, 0, 0, tiled=True)


def split_rows(x, n):
    return x.reshape(n, x.shape[0] // n, *x.shape[1:])


def lane_chunk(x, index, size):
    return lax.dynamic_slice_in_dim(x, index * size, size, axis=1)


def place_chunks(chunks, starts, like):
    out = jnp.zeros(like.shape, like.dtype)
    for chunk, start in zip(chunks, starts):
        out = lax.dynamic_update_slice_in_dim(out, chunk, start, axis=1)
    return out


def on_device(
    inputs, gate_in, gate_out, first_blocks, second_blocks, channel_blocks, group_mix, cotangent
):
    n = lax.axis_size("seq")
    m = lax.axis_size("ch")
    g_me = lax.axis_index("ch")
    rows, width = inputs.shape
    block_width = channel_blocks.shape[1]
    kq = block_width // m
    chunk_of = [(g_me + k) % m for k in range(m)]
    origin_of = [(g_me - k) % m for k in range(m)]

    mix_mine = lax.dynamic_slice_in_dim(group_mix, g_me * kq, kq, 0).astype(F32)

    def coefficient(g, h):
        return lax.dynamic_slice(mix_mine, (0, g, h), (kq, 1, 1)).reshape(1, kq)

    second_f = second_blocks.astype(F32)

    source = inputs.astype(F32)
    slope_in = jax.nn.sigmoid(gate_in * source)
    gated = (source * slope_in).astype(BF16)
    mixed_first = jnp.dot(first_blocks[0], gated, preferred_element_type=F32).astype(BF16)

    upstream = cotangent
    upstream_late, mixed_first = lax.optimization_barrier((upstream, mixed_first))
    cot_arrived = exchange([lane_chunk(upstream_late, t, kq) for t in chunk_of], "ch")
    act_grad_out = [
        sum(
            cot_arrived[k].astype(F32) * coefficient(chunk_of[p], origin_of[k])
            for k in range(m)
        ).astype(BF16)
        for p in range(m)
    ]
    act_grad_back = exchange(act_grad_out, "ch")
    act_grad = place_chunks(act_grad_back, [t * kq for t in origin_of], upstream)

    first_arrived = swap(split_rows(mixed_first, n), "seq")
    second_out = jnp.einsum(
        "cea,acd->ecd", second_f, first_arrived.astype(F32)
    ).astype(BF16)
    returned = swap(second_out, "seq").reshape(rows, width).astype(F32)
    slope_out = jax.nn.sigmoid(gate_out * source)
    hidden = (source + returned * slope_out).astype(BF16)
    pre_act = jnp.dot(hidden, channel_blocks[0], preferred_element_type=F32)
    activated = jax.nn.gelu(pre_act).astype(BF16)

    act_arrived = exchange([lane_chunk(activated, t, kq) for t in chunk_of], "ch")
    added_out = [
        sum(
            act_arrived[k].astype(F32) * coefficient(origin_of[k], chunk_of[p])
            for k in range(m)
        ).astype(BF16)
        for p in range(m)
    ]
    added_back = exchange(added_out, "ch")

    pre_grad = jax.vjp(jax.nn.gelu, pre_act)[1](act_grad.astype(F32))[0].astype(BF16)
    back_term = jnp.dot(pre_grad, channel_blocks[0].T, preferred_element_type=F32)
    hidden_grad = (upstream.astype(F32) + back_term).astype(BF16)
    channel_part = jnp.dot(hidden.T, pre_grad, preferred_element_type=F32)

    grad_flat = hidden_grad.astype(F32)
    gated_grad = (grad_flat * slope_out).astype(BF16)
    grad_arrived = swap(split_rows(gated_grad, n), "seq")
    first_out = jnp.einsum(
        "cea,ecd->acd", second_f, grad_arrived.astype(F32)
    ).astype(BF16)
    first_grad = swap(first_out, "seq").reshape(rows, width)
    first_grad, channel_part = lax.optimization_barrier((first_grad, channel_part))
    block_part = jnp.dot(first_grad, gated.T, preferred_element_type=F32)
    block_part, early_added = lax.optimization_barrier((block_part, added_back[1]))
    added_back[1] = early_added
    cq = block_part.shape[0] // m
    block_arrived = exchange(
        [lax.dynamic_slice_in_dim(block_part, t * cq, cq, 0).astype(BF16) for t in chunk_of],
        "ch",
    )
    first_block, added_back = lax.optimization_barrier((block_arrived[1], added_back))
    block_arrived[1] = first_block
    block_grad = sum(part.astype(F32) for part in block_arrived)[None]
    outputs = place_chunks(
        [
            (lane_chunk(hidden, t, kq).astype(F32) + part.astype(F32)).astype(BF16)
            for t, part in zip(origin_of, added_back)
        ],
        [t * kq for t in origin_of],
        hidden,
    )
    channel_arrived = swap(split_rows(channel_part, n).astype(BF16), "seq")
    channel_grad = jnp.sum(channel_arrived.astype(F32), axis=0)[None]

    spread = jnp.dot(first_blocks[0].T, first_grad, preferred_element_type=F32)
    input_grad = grad_flat + spread * (slope_in + gate_in * source * slope_in * (1.0 - slope_in))
    input_grad = input_grad + grad_flat * returned * slope_out * (1.0 - slope_out) * gate_out
    return (outputs, input_grad.astype(BF16), channel_grad, block_grad)


def solution(mesh):
    placed = (
        P("seq", "ch"),
        P("ch"),
        P("ch"),
        P("seq", None, None),
        P("seq", None, None),
        P("ch", None, None),
        P(),
        P("seq", "ch"),
    )
    return jax.shard_map(
        on_device,
        mesh=mesh,
        in_specs=placed,
        out_specs=(P("seq", "ch"), P("seq", "ch"), P("ch", "seq", None), P("seq", "ch", None)),
        check_vma=False,
    )
```

```python
import jax
import jax.numpy as jnp
from jax import lax
from jax.sharding import PartitionSpec as P

F32 = jnp.float32
BF16 = jnp.bfloat16


def exchange(pieces, axis_name):
    n = len(pieces)
    got = [pieces[0]]
    for k in range(1, n):
        got.append(lax.ppermute(pieces[k], axis_name, [(i, (i + k) % n) for i in range(n)]))
    return got


def swap(pieces, axis_name):
    return lax.all_to_all(pieces, axis_name, 0, 0, tiled=True)


def split_rows(x, n):
    return x.reshape(n, x.shape[0] // n, *x.shape[1:])


def lane_chunk(x, index, size):
    return lax.dynamic_slice_in_dim(x, index * size, size, axis=1)


def place_chunks(chunks, starts, like):
    out = jnp.zeros(like.shape, like.dtype)
    for chunk, start in zip(chunks, starts):
        out = lax.dynamic_update_slice_in_dim(out, chunk, start, axis=1)
    return out


def on_device(
    inputs, gate_in, gate_out, first_blocks, second_blocks, channel_blocks, group_mix, cotangent
):
    n = lax.axis_size("seq")
    m = lax.axis_size("ch")
    g_me = lax.axis_index("ch")
    rows, width = inputs.shape
    block_width = channel_blocks.shape[1]
    kq = block_width // m
    chunk_of = [(g_me + k) % m for k in range(m)]
    origin_of = [(g_me - k) % m for k in range(m)]

    mix_mine = lax.dynamic_slice_in_dim(group_mix, g_me * kq, kq, 0).astype(F32)

    def coefficient(g, h):
        return lax.dynamic_slice(mix_mine, (0, g, h), (kq, 1, 1)).reshape(1, kq)

    second_f = second_blocks.astype(F32)

    source = inputs.astype(F32)
    slope_in = jax.nn.sigmoid(gate_in * source)
    gated = (source * slope_in).astype(BF16)
    mixed_first = jnp.dot(first_blocks[0], gated, preferred_element_type=F32).astype(BF16)

    upstream = cotangent
    upstream_late, mixed_first = lax.optimization_barrier((upstream, mixed_first))
    cot_arrived = exchange([lane_chunk(upstream_late, t, kq) for t in chunk_of], "ch")
    act_grad_out = [
        sum(
            cot_arrived[k].astype(F32) * coefficient(chunk_of[p], origin_of[k])
            for k in range(m)
        ).astype(BF16)
        for p in range(m)
    ]
    act_grad_back = exchange(act_grad_out, "ch")
    act_grad = place_chunks(act_grad_back, [t * kq for t in origin_of], upstream)

    first_arrived = swap(split_rows(mixed_first, n), "seq")
    second_out = jnp.einsum(
        "cea,acd->ecd", second_f, first_arrived.astype(F32)
    ).astype(BF16)
    returned = swap(second_out, "seq").reshape(rows, width).astype(F32)
    slope_out = jax.nn.sigmoid(gate_out * source)
    hidden = (source + returned * slope_out).astype(BF16)
    pre_act = jnp.dot(hidden, channel_blocks[0], preferred_element_type=F32)
    activated = jax.nn.gelu(pre_act).astype(BF16)

    act_arrived = exchange([lane_chunk(activated, t, kq) for t in chunk_of], "ch")
    added_out = [
        sum(
            act_arrived[k].astype(F32) * coefficient(origin_of[k], chunk_of[p])
            for k in range(m)
        ).astype(BF16)
        for p in range(m)
    ]
    added_back = exchange(added_out, "ch")

    pre_grad = jax.vjp(jax.nn.gelu, pre_act)[1](act_grad.astype(F32))[0].astype(BF16)
    back_term = jnp.dot(pre_grad, channel_blocks[0].T, preferred_element_type=F32)
    hidden_grad = (upstream.astype(F32) + back_term).astype(BF16)
    channel_part = jnp.dot(hidden.T, pre_grad, preferred_element_type=F32)

    grad_flat = hidden_grad.astype(F32)
    gated_grad = (grad_flat * slope_out).astype(BF16)
    grad_arrived = swap(split_rows(gated_grad, n), "seq")
    first_out = jnp.einsum(
        "cea,ecd->acd", second_f, grad_arrived.astype(F32)
    ).astype(BF16)
    first_grad = swap(first_out, "seq").reshape(rows, width)
    input_scale = slope_in + gate_in * source * slope_in * (1.0 - slope_in)
    input_base = grad_flat + grad_flat * returned * slope_out * (1.0 - slope_out) * gate_out
    first_grad, channel_part, input_scale, input_base = lax.optimization_barrier(
        (first_grad, channel_part, input_scale, input_base)
    )
    block_part = jnp.dot(first_grad, gated.T, preferred_element_type=F32)
    cq = block_part.shape[0] // m
    block_arrived = exchange(
        [lax.dynamic_slice_in_dim(block_part, t * cq, cq, 0).astype(BF16) for t in chunk_of],
        "ch",
    )
    first_block, added_back = lax.optimization_barrier((block_arrived[1], added_back))
    block_arrived[1] = first_block
    block_grad = sum(part.astype(F32) for part in block_arrived)[None]
    outputs = place_chunks(
        [
            (lane_chunk(hidden, t, kq).astype(F32) + part.astype(F32)).astype(BF16)
            for t, part in zip(origin_of, added_back)
        ],
        [t * kq for t in origin_of],
        hidden,
    )
    channel_arrived = swap(split_rows(channel_part, n).astype(BF16), "seq")
    channel_grad = jnp.sum(channel_arrived.astype(F32), axis=0)[None]

    spread = jnp.dot(first_blocks[0].T, first_grad, preferred_element_type=F32)
    input_grad = input_base + spread * input_scale
    return (outputs, input_grad.astype(BF16), channel_grad, block_grad)


def solution(mesh):
    placed = (
        P("seq", "ch"),
        P("ch"),
        P("ch"),
        P("seq", None, None),
        P("seq", None, None),
        P("ch", None, None),
        P(),
        P("seq", "ch"),
    )
    return jax.shard_map(
        on_device,
        mesh=mesh,
        in_specs=placed,
        out_specs=(P("seq", "ch"), P("seq", "ch"), P("ch", "seq", None), P("seq", "ch", None)),
        check_vma=False,
    )
```

```python
import jax
import jax.numpy as jnp
from jax import lax
from jax.experimental.layout import Layout, with_layout_constraint
from jax.sharding import PartitionSpec as P

F32 = jnp.float32
BF16 = jnp.bfloat16


def exchange(pieces, axis_name):
    n = len(pieces)
    got = [pieces[0]]
    for k in range(1, n):
        got.append(lax.ppermute(pieces[k], axis_name, [(i, (i + k) % n) for i in range(n)]))
    return got


def swap(pieces, axis_name):
    return lax.all_to_all(pieces, axis_name, 0, 0, tiled=True)


def split_rows(x, n):
    return x.reshape(n, x.shape[0] // n, *x.shape[1:])


def lane_chunk(x, index, size):
    return lax.dynamic_slice_in_dim(x, index * size, size, axis=1)


def place_chunks(chunks, starts, like):
    out = jnp.zeros(like.shape, like.dtype)
    for chunk, start in zip(chunks, starts):
        out = lax.dynamic_update_slice_in_dim(out, chunk, start, axis=1)
    return out


def on_device(
    inputs, gate_in, gate_out, first_blocks, second_blocks, channel_blocks, group_mix, cotangent
):
    n = lax.axis_size("seq")
    m = lax.axis_size("ch")
    g_me = lax.axis_index("ch")
    rows, width = inputs.shape
    block_width = channel_blocks.shape[1]
    kq = block_width // m
    chunk_of = [(g_me + k) % m for k in range(m)]
    origin_of = [(g_me - k) % m for k in range(m)]

    mix_mine = lax.dynamic_slice_in_dim(group_mix, g_me * kq, kq, 0).astype(F32)

    def coefficient(g, h):
        return lax.dynamic_slice(mix_mine, (0, g, h), (kq, 1, 1)).reshape(1, kq)

    second_f = second_blocks.astype(F32)

    source = inputs.astype(F32)
    slope_in = jax.nn.sigmoid(gate_in * source)
    gated = (source * slope_in).astype(BF16)
    mixed_first = jnp.dot(first_blocks[0], gated, preferred_element_type=F32).astype(BF16)
    mixed_first = with_layout_constraint(mixed_first, Layout(major_to_minor=(0, 1)))

    upstream = cotangent
    upstream_late, mixed_first = lax.optimization_barrier((upstream, mixed_first))
    cot_arrived = exchange([lane_chunk(upstream_late, t, kq) for t in chunk_of], "ch")
    act_grad_out = [
        sum(
            cot_arrived[k].astype(F32) * coefficient(chunk_of[p], origin_of[k])
            for k in range(m)
        ).astype(BF16)
        for p in range(m)
    ]
    act_grad_back = exchange(act_grad_out, "ch")
    act_grad = place_chunks(act_grad_back, [t * kq for t in origin_of], upstream)

    first_arrived = swap(split_rows(mixed_first, n), "seq")
    second_out = jnp.einsum(
        "cea,acd->ecd", second_f, first_arrived.astype(F32)
    ).astype(BF16)
    returned = swap(second_out, "seq").reshape(rows, width).astype(F32)
    slope_out = jax.nn.sigmoid(gate_out * source)
    hidden = (source + returned * slope_out).astype(BF16)
    pre_act = jnp.dot(hidden, channel_blocks[0], preferred_element_type=F32)
    activated = jax.nn.gelu(pre_act).astype(BF16)

    act_arrived = exchange([lane_chunk(activated, t, kq) for t in chunk_of], "ch")
    added_out = [
        sum(
            act_arrived[k].astype(F32) * coefficient(origin_of[k], chunk_of[p])
            for k in range(m)
        ).astype(BF16)
        for p in range(m)
    ]
    added_back = exchange(added_out, "ch")

    pre_grad = jax.vjp(jax.nn.gelu, pre_act)[1](act_grad.astype(F32))[0].astype(BF16)
    back_term = jnp.dot(pre_grad, channel_blocks[0].T, preferred_element_type=F32)
    hidden_grad = (upstream.astype(F32) + back_term).astype(BF16)
    channel_part = jnp.dot(hidden.T, pre_grad, preferred_element_type=F32)

    grad_flat = hidden_grad.astype(F32)
    gated_grad = (grad_flat * slope_out).astype(BF16)
    grad_arrived = swap(split_rows(gated_grad, n), "seq")
    first_out = jnp.einsum(
        "cea,ecd->acd", second_f, grad_arrived.astype(F32)
    ).astype(BF16)
    first_grad = swap(first_out, "seq").reshape(rows, width)
    first_grad, channel_part = lax.optimization_barrier((first_grad, channel_part))
    block_part = jnp.dot(first_grad, gated.T, preferred_element_type=F32)
    cq = block_part.shape[0] // m
    block_arrived = exchange(
        [lax.dynamic_slice_in_dim(block_part, t * cq, cq, 0).astype(BF16) for t in chunk_of],
        "ch",
    )
    first_block, added_back = lax.optimization_barrier((block_arrived[1], added_back))
    block_arrived[1] = first_block
    block_grad = sum(part.astype(F32) for part in block_arrived)[None]
    outputs = place_chunks(
        [
            (lane_chunk(hidden, t, kq).astype(F32) + part.astype(F32)).astype(BF16)
            for t, part in zip(origin_of, added_back)
        ],
        [t * kq for t in origin_of],
        hidden,
    )
    channel_arrived = swap(split_rows(channel_part, n).astype(BF16), "seq")
    channel_grad = jnp.sum(channel_arrived.astype(F32), axis=0)[None]

    spread = jnp.dot(first_blocks[0].T, first_grad, preferred_element_type=F32)
    input_grad = grad_flat + spread * (slope_in + gate_in * source * slope_in * (1.0 - slope_in))
    input_grad = input_grad + grad_flat * returned * slope_out * (1.0 - slope_out) * gate_out
    return (outputs, input_grad.astype(BF16), channel_grad, block_grad)


def solution(mesh):
    placed = (
        P("seq", "ch"),
        P("ch"),
        P("ch"),
        P("seq", None, None),
        P("seq", None, None),
        P("ch", None, None),
        P(),
        P("seq", "ch"),
    )
    return jax.shard_map(
        on_device,
        mesh=mesh,
        in_specs=placed,
        out_specs=(P("seq", "ch"), P("seq", "ch"), P("ch", "seq", None), P("seq", "ch", None)),
        check_vma=False,
    )
```

```python
import jax
import jax.numpy as jnp
from jax import lax
from jax.sharding import PartitionSpec as P

F32 = jnp.float32
BF16 = jnp.bfloat16


def exchange(pieces, axis_name):
    n = len(pieces)
    got = [pieces[0]]
    for k in range(1, n):
        got.append(lax.ppermute(pieces[k], axis_name, [(i, (i + k) % n) for i in range(n)]))
    return got


def swap(pieces, axis_name):
    return lax.all_to_all(pieces, axis_name, 0, 0, tiled=True)


def split_rows(x, n):
    return x.reshape(n, x.shape[0] // n, *x.shape[1:])


def lane_chunk(x, index, size):
    return lax.dynamic_slice_in_dim(x, index * size, size, axis=1)


def place_chunks(chunks, starts, like):
    out = jnp.zeros(like.shape, like.dtype)
    for chunk, start in zip(chunks, starts):
        out = lax.dynamic_update_slice_in_dim(out, chunk, start, axis=1)
    return out


def on_device(
    inputs, gate_in, gate_out, first_blocks, second_blocks, channel_blocks, group_mix, cotangent
):
    n = lax.axis_size("seq")
    m = lax.axis_size("ch")
    g_me = lax.axis_index("ch")
    rows, width = inputs.shape
    block_width = channel_blocks.shape[1]
    kq = block_width // m
    chunk_of = [(g_me + k) % m for k in range(m)]
    origin_of = [(g_me - k) % m for k in range(m)]

    mix_mine = lax.dynamic_slice_in_dim(group_mix, g_me * kq, kq, 0).astype(F32)

    def coefficient(g, h):
        return lax.dynamic_slice(mix_mine, (0, g, h), (kq, 1, 1)).reshape(1, kq)

    second_f = second_blocks.astype(F32)

    source = inputs.astype(F32)
    slope_in = jax.nn.sigmoid(gate_in * source)
    gated = (source * slope_in).astype(BF16)
    mixed_first = jnp.dot(first_blocks[0], gated, preferred_element_type=F32).astype(BF16)

    upstream = cotangent
    upstream_late, mixed_first = lax.optimization_barrier((upstream, mixed_first))
    cot_arrived = exchange([lane_chunk(upstream_late, t, kq) for t in chunk_of], "ch")
    act_grad_out = [
        sum(
            cot_arrived[k].astype(F32) * coefficient(chunk_of[p], origin_of[k])
            for k in range(m)
        ).astype(BF16)
        for p in range(m)
    ]
    act_grad_back = exchange(act_grad_out, "ch")
    act_grad = place_chunks(act_grad_back, [t * kq for t in origin_of], upstream)

    first_arrived = swap(split_rows(mixed_first, n), "seq")
    second_out = jnp.einsum(
        "cea,acd->ecd", second_f, first_arrived.astype(F32)
    ).astype(BF16)
    returned = swap(second_out, "seq").reshape(rows, width).astype(F32)
    slope_out = jax.nn.sigmoid(gate_out * source)
    hidden = (source + returned * slope_out).astype(BF16)
    pre_act = jnp.dot(hidden, channel_blocks[0], preferred_element_type=F32)
    activated = jax.nn.gelu(pre_act).astype(BF16)

    act_arrived = exchange([lane_chunk(activated, t, kq) for t in chunk_of], "ch")
    added_out = [
        sum(
            act_arrived[k].astype(F32) * coefficient(origin_of[k], chunk_of[p])
            for k in range(m)
        ).astype(BF16)
        for p in range(m)
    ]
    added_back = exchange(added_out, "ch")

    pre_grad = jax.vjp(jax.nn.gelu, pre_act)[1](act_grad.astype(F32))[0].astype(BF16)
    back_term = jnp.dot(pre_grad, channel_blocks[0].T, preferred_element_type=F32)
    hidden_grad = (upstream.astype(F32) + back_term).astype(BF16)
    channel_part = jnp.dot(hidden.T, pre_grad, preferred_element_type=F32)

    grad_flat = hidden_grad.astype(F32)
    gated_grad = (grad_flat * slope_out).astype(BF16)
    grad_arrived = swap(split_rows(gated_grad, n), "seq")
    first_out = jnp.einsum(
        "cea,ecd->acd", second_f, grad_arrived.astype(F32)
    ).astype(BF16)
    first_grad = swap(first_out, "seq").reshape(rows, width)
    first_grad, channel_part = lax.optimization_barrier((first_grad, channel_part))
    block_part = jnp.dot(first_grad, gated.T, preferred_element_type=F32)
    cq = block_part.shape[0] // m
    block_arrived = exchange(
        [lax.dynamic_slice_in_dim(block_part, t * cq, cq, 0).astype(BF16) for t in chunk_of],
        "ch",
    )
    first_block, added_back, spread_source = lax.optimization_barrier(
        (block_arrived[1], added_back, first_grad)
    )
    block_arrived[1] = first_block
    block_grad = sum(part.astype(F32) for part in block_arrived)[None]
    outputs = place_chunks(
        [
            (lane_chunk(hidden, t, kq).astype(F32) + part.astype(F32)).astype(BF16)
            for t, part in zip(origin_of, added_back)
        ],
        [t * kq for t in origin_of],
        hidden,
    )
    channel_arrived = swap(split_rows(channel_part, n).astype(BF16), "seq")
    channel_grad = jnp.sum(channel_arrived.astype(F32), axis=0)[None]

    spread = jnp.dot(first_blocks[0].T, spread_source, preferred_element_type=F32)
    input_grad = grad_flat + spread * (slope_in + gate_in * source * slope_in * (1.0 - slope_in))
    input_grad = input_grad + grad_flat * returned * slope_out * (1.0 - slope_out) * gate_out
    return (outputs, input_grad.astype(BF16), channel_grad, block_grad)


def solution(mesh):
    placed = (
        P("seq", "ch"),
        P("ch"),
        P("ch"),
        P("seq", None, None),
        P("seq", None, None),
        P("ch", None, None),
        P(),
        P("seq", "ch"),
    )
    return jax.shard_map(
        on_device,
        mesh=mesh,
        in_specs=placed,
        out_specs=(P("seq", "ch"), P("seq", "ch"), P("ch", "seq", None), P("seq", "ch", None)),
        check_vma=False,
    )
```

```python
import jax
import jax.numpy as jnp
from jax import lax
from jax.sharding import PartitionSpec as P

F32 = jnp.float32
BF16 = jnp.bfloat16


def exchange(pieces, axis_name):
    n = len(pieces)
    got = [pieces[0]]
    for k in range(1, n):
        got.append(lax.ppermute(pieces[k], axis_name, [(i, (i + k) % n) for i in range(n)]))
    return got


def swap(pieces, axis_name):
    return lax.all_to_all(pieces, axis_name, 0, 0, tiled=True)


def split_rows(x, n):
    return x.reshape(n, x.shape[0] // n, *x.shape[1:])


def lane_chunk(x, index, size):
    return lax.dynamic_slice_in_dim(x, index * size, size, axis=1)


def place_chunks(chunks, starts, like):
    out = jnp.zeros(like.shape, like.dtype)
    for chunk, start in zip(chunks, starts):
        out = lax.dynamic_update_slice_in_dim(out, chunk, start, axis=1)
    return out


def on_device(
    inputs, gate_in, gate_out, first_blocks, second_blocks, channel_blocks, group_mix, cotangent
):
    n = lax.axis_size("seq")
    m = lax.axis_size("ch")
    g_me = lax.axis_index("ch")
    rows, width = inputs.shape
    block_width = channel_blocks.shape[1]
    kq = block_width // m
    chunk_of = [(g_me + k) % m for k in range(m)]
    origin_of = [(g_me - k) % m for k in range(m)]

    mix_mine = lax.dynamic_slice_in_dim(group_mix, g_me * kq, kq, 0).astype(F32)

    def coefficient(g, h):
        return lax.dynamic_slice(mix_mine, (0, g, h), (kq, 1, 1)).reshape(1, kq)

    second_f = second_blocks.astype(F32)

    source = inputs.astype(F32)
    slope_in = jax.nn.sigmoid(gate_in * source)
    gated = (source * slope_in).astype(BF16)
    mixed_first = jnp.dot(first_blocks[0], gated, preferred_element_type=F32).astype(BF16)

    upstream = cotangent
    upstream_late, mixed_first = lax.optimization_barrier((upstream, mixed_first))
    cot_arrived = exchange([lane_chunk(upstream_late, t, kq) for t in chunk_of], "ch")
    act_grad_out = [
        sum(
            cot_arrived[k].astype(F32) * coefficient(chunk_of[p], origin_of[k])
            for k in range(m)
        ).astype(BF16)
        for p in range(m)
    ]
    act_grad_back = exchange(act_grad_out, "ch")
    act_grad = place_chunks(act_grad_back, [t * kq for t in origin_of], upstream)

    first_arrived = swap(split_rows(mixed_first, n), "seq")
    second_out = jnp.einsum(
        "cea,acd->ecd", second_f, first_arrived.astype(F32)
    ).astype(BF16)
    returned = swap(second_out, "seq").reshape(rows, width).astype(F32)
    slope_out = jax.nn.sigmoid(gate_out * source)
    hidden = (source + returned * slope_out).astype(BF16)
    pre_act = jnp.dot(hidden, channel_blocks[0], preferred_element_type=F32)
    activated = jax.nn.gelu(pre_act).astype(BF16)

    act_arrived = exchange([lane_chunk(activated, t, kq) for t in chunk_of], "ch")
    added_out = [
        sum(
            act_arrived[k].astype(F32) * coefficient(origin_of[k], chunk_of[p])
            for k in range(m)
        ).astype(BF16)
        for p in range(m)
    ]
    added_back = exchange(added_out, "ch")

    pre_grad = jax.vjp(jax.nn.gelu, pre_act)[1](act_grad.astype(F32))[0].astype(BF16)
    back_term = jnp.dot(pre_grad, channel_blocks[0].T, preferred_element_type=F32)
    hidden_grad = (upstream.astype(F32) + back_term).astype(BF16)
    channel_part = jnp.dot(hidden.T, pre_grad, preferred_element_type=F32)

    grad_flat = hidden_grad.astype(F32)
    gated_grad = (grad_flat * slope_out).astype(BF16)
    grad_arrived = swap(split_rows(gated_grad, n), "seq")
    first_out = jnp.einsum(
        "cea,ecd->acd", second_f, grad_arrived.astype(F32)
    ).astype(BF16)
    first_grad = swap(first_out, "seq").reshape(rows, width)
    first_grad, channel_part = lax.optimization_barrier((first_grad, channel_part))
    block_part = jnp.dot(first_grad, gated.T, preferred_element_type=F32)
    cq = block_part.shape[0] // m
    block_arrived = exchange(
        [lax.dynamic_slice_in_dim(block_part, t * cq, cq, 0).astype(BF16) for t in chunk_of],
        "ch",
    )
    first_block, added_back = lax.optimization_barrier((block_arrived[1], added_back))
    block_arrived[1] = first_block
    outputs = place_chunks(
        [
            (lane_chunk(hidden, t, kq).astype(F32) + part.astype(F32)).astype(BF16)
            for t, part in zip(origin_of, added_back)
        ],
        [t * kq for t in origin_of],
        hidden,
    )
    channel_arrived = swap(split_rows(channel_part, n).astype(BF16), "seq")
    channel_grad = jnp.sum(channel_arrived.astype(F32), axis=0)[None]
    late_blocks, channel_grad = lax.optimization_barrier((block_arrived[2:], channel_grad))
    block_arrived[2:] = late_blocks
    block_grad = sum(part.astype(F32) for part in block_arrived)[None]

    spread = jnp.dot(first_blocks[0].T, first_grad, preferred_element_type=F32)
    input_grad = grad_flat + spread * (slope_in + gate_in * source * slope_in * (1.0 - slope_in))
    input_grad = input_grad + grad_flat * returned * slope_out * (1.0 - slope_out) * gate_out
    return (outputs, input_grad.astype(BF16), channel_grad, block_grad)


def solution(mesh):
    placed = (
        P("seq", "ch"),
        P("ch"),
        P("ch"),
        P("seq", None, None),
        P("seq", None, None),
        P("ch", None, None),
        P(),
        P("seq", "ch"),
    )
    return jax.shard_map(
        on_device,
        mesh=mesh,
        in_specs=placed,
        out_specs=(P("seq", "ch"), P("seq", "ch"), P("ch", "seq", None), P("seq", "ch", None)),
        check_vma=False,
    )
```

```python
import jax
import jax.numpy as jnp
from jax import lax
from jax.sharding import PartitionSpec as P

F32 = jnp.float32
BF16 = jnp.bfloat16


def exchange(pieces, axis_name):
    n = len(pieces)
    got = [pieces[0]]
    for k in range(1, n):
        got.append(lax.ppermute(pieces[k], axis_name, [(i, (i + k) % n) for i in range(n)]))
    return got


def swap(pieces, axis_name):
    return lax.all_to_all(pieces, axis_name, 0, 0, tiled=True)


def split_rows(x, n):
    return x.reshape(n, x.shape[0] // n, *x.shape[1:])


def lane_chunk(x, index, size):
    return lax.dynamic_slice_in_dim(x, index * size, size, axis=1)


def place_chunks(chunks, starts, like):
    out = jnp.zeros(like.shape, like.dtype)
    for chunk, start in zip(chunks, starts):
        out = lax.dynamic_update_slice_in_dim(out, chunk, start, axis=1)
    return out


def on_device(
    inputs, gate_in, gate_out, first_blocks, second_blocks, channel_blocks, group_mix, cotangent
):
    n = lax.axis_size("seq")
    m = lax.axis_size("ch")
    g_me = lax.axis_index("ch")
    rows, width = inputs.shape
    block_width = channel_blocks.shape[1]
    kq = block_width // m
    chunk_of = [(g_me + k) % m for k in range(m)]
    origin_of = [(g_me - k) % m for k in range(m)]

    mix_mine = lax.dynamic_slice_in_dim(group_mix, g_me * kq, kq, 0).astype(F32)

    def coefficient(g, h):
        return lax.dynamic_slice(mix_mine, (0, g, h), (kq, 1, 1)).reshape(1, kq)

    cq_seq = second_blocks.shape[0]
    diagonal = jnp.eye(cq_seq, dtype=BF16)
    seq_mix = (jnp.transpose(second_blocks, (1, 0, 2))[:, :, :, None] * diagonal[None, :, None, :])
    seq_mix = seq_mix.reshape(n * cq_seq, n * cq_seq)

    source = inputs.astype(F32)
    slope_in = jax.nn.sigmoid(gate_in * source)
    gated = (source * slope_in).astype(BF16)
    mixed_first = jnp.dot(first_blocks[0], gated, preferred_element_type=F32).astype(BF16)

    upstream = cotangent
    upstream_late, mixed_first = lax.optimization_barrier((upstream, mixed_first))
    cot_arrived = exchange([lane_chunk(upstream_late, t, kq) for t in chunk_of], "ch")
    act_grad_out = [
        sum(
            cot_arrived[k].astype(F32) * coefficient(chunk_of[p], origin_of[k])
            for k in range(m)
        ).astype(BF16)
        for p in range(m)
    ]
    act_grad_back = exchange(act_grad_out, "ch")
    act_grad = place_chunks(act_grad_back, [t * kq for t in origin_of], upstream)

    first_arrived = swap(split_rows(mixed_first, n), "seq")
    second_out = jnp.dot(
        seq_mix, first_arrived.reshape(rows, width), preferred_element_type=F32
    ).astype(BF16).reshape(n, cq_seq, width)
    returned = swap(second_out, "seq").reshape(rows, width).astype(F32)
    slope_out = jax.nn.sigmoid(gate_out * source)
    hidden = (source + returned * slope_out).astype(BF16)
    pre_act = jnp.dot(hidden, channel_blocks[0], preferred_element_type=F32)
    activated = jax.nn.gelu(pre_act).astype(BF16)

    act_arrived = exchange([lane_chunk(activated, t, kq) for t in chunk_of], "ch")
    added_out = [
        sum(
            act_arrived[k].astype(F32) * coefficient(origin_of[k], chunk_of[p])
            for k in range(m)
        ).astype(BF16)
        for p in range(m)
    ]
    added_back = exchange(added_out, "ch")

    pre_grad = jax.vjp(jax.nn.gelu, pre_act)[1](act_grad.astype(F32))[0].astype(BF16)
    back_term = jnp.dot(pre_grad, channel_blocks[0].T, preferred_element_type=F32)
    hidden_grad = (upstream.astype(F32) + back_term).astype(BF16)
    channel_part = jnp.dot(hidden.T, pre_grad, preferred_element_type=F32)

    grad_flat = hidden_grad.astype(F32)
    gated_grad = (grad_flat * slope_out).astype(BF16)
    grad_arrived = swap(split_rows(gated_grad, n), "seq")
    first_out = jnp.dot(
        seq_mix.T, grad_arrived.reshape(rows, width), preferred_element_type=F32
    ).astype(BF16).reshape(n, cq_seq, width)
    first_grad = swap(first_out, "seq").reshape(rows, width)
    first_grad, channel_part = lax.optimization_barrier((first_grad, channel_part))
    block_part = jnp.dot(first_grad, gated.T, preferred_element_type=F32)
    cq = block_part.shape[0] // m
    block_arrived = exchange(
        [lax.dynamic_slice_in_dim(block_part, t * cq, cq, 0).astype(BF16) for t in chunk_of],
        "ch",
    )
    first_block, added_back = lax.optimization_barrier((block_arrived[1], added_back))
    block_arrived[1] = first_block
    block_grad = sum(part.astype(F32) for part in block_arrived)[None]
    outputs = place_chunks(
        [
            (lane_chunk(hidden, t, kq).astype(F32) + part.astype(F32)).astype(BF16)
            for t, part in zip(origin_of, added_back)
        ],
        [t * kq for t in origin_of],
        hidden,
    )
    channel_arrived = swap(split_rows(channel_part, n).astype(BF16), "seq")
    channel_grad = jnp.sum(channel_arrived.astype(F32), axis=0)[None]

    spread = jnp.dot(first_blocks[0].T, first_grad, preferred_element_type=F32)
    input_grad = grad_flat + spread * (slope_in + gate_in * source * slope_in * (1.0 - slope_in))
    input_grad = input_grad + grad_flat * returned * slope_out * (1.0 - slope_out) * gate_out
    return (outputs, input_grad.astype(BF16), channel_grad, block_grad)


def solution(mesh):
    placed = (
        P("seq", "ch"),
        P("ch"),
        P("ch"),
        P("seq", None, None),
        P("seq", None, None),
        P("ch", None, None),
        P(),
        P("seq", "ch"),
    )
    return jax.shard_map(
        on_device,
        mesh=mesh,
        in_specs=placed,
        out_specs=(P("seq", "ch"), P("seq", "ch"), P("ch", "seq", None), P("seq", "ch", None)),
        check_vma=False,
    )
```

```python
import jax
import jax.numpy as jnp
from jax import lax
from jax.experimental.layout import Layout, with_layout_constraint
from jax.sharding import PartitionSpec as P

F32 = jnp.float32
BF16 = jnp.bfloat16


def exchange(pieces, axis_name):
    n = len(pieces)
    got = [pieces[0]]
    for k in range(1, n):
        got.append(lax.ppermute(pieces[k], axis_name, [(i, (i + k) % n) for i in range(n)]))
    return got


def swap(pieces, axis_name):
    return lax.all_to_all(pieces, axis_name, 0, 0, tiled=True)


def split_rows(x, n):
    return x.reshape(n, x.shape[0] // n, *x.shape[1:])


def lane_chunk(x, index, size):
    return lax.dynamic_slice_in_dim(x, index * size, size, axis=1)


def place_chunks(chunks, starts, like):
    out = jnp.zeros(like.shape, like.dtype)
    for chunk, start in zip(chunks, starts):
        out = lax.dynamic_update_slice_in_dim(out, chunk, start, axis=1)
    return out


def on_device(
    inputs, gate_in, gate_out, first_blocks, second_blocks, channel_blocks, group_mix, cotangent
):
    n = lax.axis_size("seq")
    m = lax.axis_size("ch")
    g_me = lax.axis_index("ch")
    rows, width = inputs.shape
    block_width = channel_blocks.shape[1]
    kq = block_width // m
    chunk_of = [(g_me + k) % m for k in range(m)]
    origin_of = [(g_me - k) % m for k in range(m)]

    mix_mine = lax.dynamic_slice_in_dim(group_mix, g_me * kq, kq, 0).astype(F32)

    def coefficient(g, h):
        return lax.dynamic_slice(mix_mine, (0, g, h), (kq, 1, 1)).reshape(1, kq)

    cq_seq = second_blocks.shape[0]
    diagonal = jnp.eye(cq_seq, dtype=BF16)

    source = inputs.astype(F32)
    slope_in = jax.nn.sigmoid(gate_in * source)
    gated = (source * slope_in).astype(BF16)
    mixed_first = jnp.dot(first_blocks[0], gated, preferred_element_type=F32).astype(BF16)
    mixed_first = with_layout_constraint(mixed_first, Layout(major_to_minor=(0, 1)))
    second_late, mixed_first = lax.optimization_barrier((second_blocks, mixed_first))
    seq_mix = (jnp.transpose(second_late, (1, 0, 2))[:, :, :, None] * diagonal[None, :, None, :])
    seq_mix = seq_mix.reshape(n * cq_seq, n * cq_seq)

    upstream = cotangent
    upstream_late, mixed_first = lax.optimization_barrier((upstream, mixed_first))
    cot_arrived = exchange([lane_chunk(upstream_late, t, kq) for t in chunk_of], "ch")
    act_grad_out = [
        sum(
            cot_arrived[k].astype(F32) * coefficient(chunk_of[p], origin_of[k])
            for k in range(m)
        ).astype(BF16)
        for p in range(m)
    ]
    act_grad_back = exchange(act_grad_out, "ch")
    act_grad = place_chunks(act_grad_back, [t * kq for t in origin_of], upstream)

    first_arrived = swap(split_rows(mixed_first, n), "seq")
    second_out = jnp.dot(
        seq_mix, first_arrived.reshape(rows, width), preferred_element_type=F32
    ).astype(BF16).reshape(n, cq_seq, width)
    returned = swap(second_out, "seq").reshape(rows, width).astype(F32)
    slope_out = jax.nn.sigmoid(gate_out * source)
    hidden = (source + returned * slope_out).astype(BF16)
    pre_act = jnp.dot(hidden, channel_blocks[0], preferred_element_type=F32)
    activated = jax.nn.gelu(pre_act).astype(BF16)

    act_arrived = exchange([lane_chunk(activated, t, kq) for t in chunk_of], "ch")
    added_out = [
        sum(
            act_arrived[k].astype(F32) * coefficient(origin_of[k], chunk_of[p])
            for k in range(m)
        ).astype(BF16)
        for p in range(m)
    ]
    added_back = exchange(added_out, "ch")

    pre_grad = jax.vjp(jax.nn.gelu, pre_act)[1](act_grad.astype(F32))[0].astype(BF16)
    back_term = jnp.dot(pre_grad, channel_blocks[0].T, preferred_element_type=F32)
    hidden_grad = (upstream.astype(F32) + back_term).astype(BF16)
    channel_part = jnp.dot(hidden.T, pre_grad, preferred_element_type=F32)

    grad_flat = hidden_grad.astype(F32)
    gated_grad = (grad_flat * slope_out).astype(BF16)
    grad_arrived = swap(split_rows(gated_grad, n), "seq")
    first_out = jnp.dot(
        seq_mix.T, grad_arrived.reshape(rows, width), preferred_element_type=F32
    ).astype(BF16).reshape(n, cq_seq, width)
    first_grad = swap(first_out, "seq").reshape(rows, width)
    first_grad, channel_part = lax.optimization_barrier((first_grad, channel_part))
    block_part = jnp.dot(first_grad, gated.T, preferred_element_type=F32)
    cq = block_part.shape[0] // m
    block_arrived = exchange(
        [lax.dynamic_slice_in_dim(block_part, t * cq, cq, 0).astype(BF16) for t in chunk_of],
        "ch",
    )
    first_block, added_back = lax.optimization_barrier((block_arrived[1], added_back))
    block_arrived[1] = first_block
    block_grad = sum(part.astype(F32) for part in block_arrived)[None]
    outputs = place_chunks(
        [
            (lane_chunk(hidden, t, kq).astype(F32) + part.astype(F32)).astype(BF16)
            for t, part in zip(origin_of, added_back)
        ],
        [t * kq for t in origin_of],
        hidden,
    )
    channel_arrived = swap(split_rows(channel_part, n).astype(BF16), "seq")
    channel_grad = jnp.sum(channel_arrived.astype(F32), axis=0)[None]

    spread = jnp.dot(first_blocks[0].T, first_grad, preferred_element_type=F32)
    input_grad = grad_flat + spread * (slope_in + gate_in * source * slope_in * (1.0 - slope_in))
    input_grad = input_grad + grad_flat * returned * slope_out * (1.0 - slope_out) * gate_out
    return (outputs, input_grad.astype(BF16), channel_grad, block_grad)


def solution(mesh):
    placed = (
        P("seq", "ch"),
        P("ch"),
        P("ch"),
        P("seq", None, None),
        P("seq", None, None),
        P("ch", None, None),
        P(),
        P("seq", "ch"),
    )
    return jax.shard_map(
        on_device,
        mesh=mesh,
        in_specs=placed,
        out_specs=(P("seq", "ch"), P("seq", "ch"), P("ch", "seq", None), P("seq", "ch", None)),
        check_vma=False,
    )
```

```python
import jax
import jax.numpy as jnp
from jax import lax
from jax.sharding import PartitionSpec as P

F32 = jnp.float32
BF16 = jnp.bfloat16


def exchange(pieces, axis_name):
    n = len(pieces)
    got = [pieces[0]]
    for k in range(1, n):
        got.append(lax.ppermute(pieces[k], axis_name, [(i, (i + k) % n) for i in range(n)]))
    return got


def swap(pieces, axis_name):
    return lax.all_to_all(pieces, axis_name, 0, 0, tiled=True)


def split_rows(x, n):
    return x.reshape(n, x.shape[0] // n, *x.shape[1:])


def lane_chunk(x, index, size):
    return lax.dynamic_slice_in_dim(x, index * size, size, axis=1)


def place_chunks(chunks, starts, like):
    out = jnp.zeros(like.shape, like.dtype)
    for chunk, start in zip(chunks, starts):
        out = lax.dynamic_update_slice_in_dim(out, chunk, start, axis=1)
    return out


def on_device(
    inputs, gate_in, gate_out, first_blocks, second_blocks, channel_blocks, group_mix, cotangent
):
    n = lax.axis_size("seq")
    m = lax.axis_size("ch")
    g_me = lax.axis_index("ch")
    rows, width = inputs.shape
    block_width = channel_blocks.shape[1]
    kq = block_width // m
    chunk_of = [(g_me + k) % m for k in range(m)]
    origin_of = [(g_me - k) % m for k in range(m)]

    mix_mine = lax.dynamic_slice_in_dim(group_mix, g_me * kq, kq, 0).astype(F32)

    def coefficient(g, h):
        return lax.dynamic_slice(mix_mine, (0, g, h), (kq, 1, 1)).reshape(1, kq)

    second_f = second_blocks.astype(F32)

    source = inputs.astype(F32)
    slope_in = jax.nn.sigmoid(gate_in * source)
    gated = (source * slope_in).astype(BF16)
    mixed_first = jnp.dot(first_blocks[0], gated, preferred_element_type=F32).astype(BF16)

    upstream = cotangent
    upstream_late, mixed_first = lax.optimization_barrier((upstream, mixed_first))
    cot_arrived = exchange([lane_chunk(upstream_late, t, kq) for t in chunk_of], "ch")
    act_grad_out = [
        sum(
            cot_arrived[k].astype(F32) * coefficient(chunk_of[p], origin_of[k])
            for k in range(m)
        ).astype(BF16)
        for p in range(m)
    ]
    act_grad_back = exchange(act_grad_out, "ch")
    act_grad = place_chunks(act_grad_back, [t * kq for t in origin_of], upstream)

    first_arrived = swap(split_rows(mixed_first, n), "seq")
    second_out = jnp.einsum(
        "cea,acd->ecd", second_f, first_arrived.astype(F32)
    ).astype(BF16)
    returned = swap(second_out, "seq").reshape(rows, width).astype(F32)
    slope_out = jax.nn.sigmoid(gate_out * source)
    hidden = (source + returned * slope_out).astype(BF16)
    pre_act = jnp.dot(hidden, channel_blocks[0], preferred_element_type=F32)
    activated = jax.nn.gelu(pre_act).astype(BF16)

    act_arrived = exchange([lane_chunk(activated, t, kq) for t in chunk_of], "ch")
    added_out = [
        sum(
            act_arrived[k].astype(F32) * coefficient(origin_of[k], chunk_of[p])
            for k in range(m)
        ).astype(BF16)
        for p in range(m)
    ]
    added_back = exchange(added_out, "ch")

    pre_grad = jax.vjp(jax.nn.gelu, pre_act)[1](act_grad.astype(F32))[0].astype(BF16)
    back_term = jnp.dot(pre_grad, channel_blocks[0].T, preferred_element_type=F32)
    hidden_grad = (upstream.astype(F32) + back_term).astype(BF16)
    channel_part = jnp.dot(hidden.T, pre_grad, preferred_element_type=F32)

    grad_flat = hidden_grad.astype(F32)
    gated_grad = (grad_flat * slope_out).astype(BF16)
    grad_arrived = swap(split_rows(gated_grad, n), "seq")
    first_out = jnp.einsum(
        "cea,ecd->acd", second_f, grad_arrived.astype(F32)
    ).astype(BF16)
    first_grad = swap(first_out, "seq").reshape(rows, width)
    first_grad, channel_part = lax.optimization_barrier((first_grad, channel_part))
    block_part = jnp.dot(first_grad, gated.T, preferred_element_type=F32)
    cq = block_part.shape[0] // m
    block_arrived = exchange(
        [lax.dynamic_slice_in_dim(block_part, t * cq, cq, 0).astype(BF16) for t in chunk_of],
        "ch",
    )
    first_block, added_back = lax.optimization_barrier((block_arrived[1], added_back))
    (early_sum,) = lax.optimization_barrier(
        (block_arrived[0].astype(F32) + first_block.astype(F32),)
    )
    block_grad = (early_sum + block_arrived[2].astype(F32) + block_arrived[3].astype(F32))[None]
    outputs = place_chunks(
        [
            (lane_chunk(hidden, t, kq).astype(F32) + part.astype(F32)).astype(BF16)
            for t, part in zip(origin_of, added_back)
        ],
        [t * kq for t in origin_of],
        hidden,
    )
    channel_arrived = swap(split_rows(channel_part, n).astype(BF16), "seq")
    channel_grad = jnp.sum(channel_arrived.astype(F32), axis=0)[None]

    spread = jnp.dot(first_blocks[0].T, first_grad, preferred_element_type=F32)
    input_grad = grad_flat + spread * (slope_in + gate_in * source * slope_in * (1.0 - slope_in))
    input_grad = input_grad + grad_flat * returned * slope_out * (1.0 - slope_out) * gate_out
    return (outputs, input_grad.astype(BF16), channel_grad, block_grad)


def solution(mesh):
    placed = (
        P("seq", "ch"),
        P("ch"),
        P("ch"),
        P("seq", None, None),
        P("seq", None, None),
        P("ch", None, None),
        P(),
        P("seq", "ch"),
    )
    return jax.shard_map(
        on_device,
        mesh=mesh,
        in_specs=placed,
        out_specs=(P("seq", "ch"), P("seq", "ch"), P("ch", "seq", None), P("seq", "ch", None)),
        check_vma=False,
    )
```

```python
import jax
import jax.numpy as jnp
from jax import lax
from jax.sharding import PartitionSpec as P

F32 = jnp.float32
BF16 = jnp.bfloat16


def exchange(pieces, axis_name):
    n = len(pieces)
    got = [pieces[0]]
    for k in range(1, n):
        got.append(lax.ppermute(pieces[k], axis_name, [(i, (i + k) % n) for i in range(n)]))
    return got


def swap(pieces, axis_name):
    return lax.all_to_all(pieces, axis_name, 0, 0, tiled=True)


def split_rows(x, n):
    return x.reshape(n, x.shape[0] // n, *x.shape[1:])


def lane_chunk(x, index, size):
    return lax.dynamic_slice_in_dim(x, index * size, size, axis=1)


def place_chunks(chunks, starts, like):
    out = jnp.zeros(like.shape, like.dtype)
    for chunk, start in zip(chunks, starts):
        out = lax.dynamic_update_slice_in_dim(out, chunk, start, axis=1)
    return out


def on_device(
    inputs, gate_in, gate_out, first_blocks, second_blocks, channel_blocks, group_mix, cotangent
):
    n = lax.axis_size("seq")
    m = lax.axis_size("ch")
    g_me = lax.axis_index("ch")
    rows, width = inputs.shape
    block_width = channel_blocks.shape[1]
    kq = block_width // m
    chunk_of = [(g_me + k) % m for k in range(m)]
    origin_of = [(g_me - k) % m for k in range(m)]

    mix_mine = lax.dynamic_slice_in_dim(group_mix, g_me * kq, kq, 0).astype(F32)

    def coefficient(g, h):
        return lax.dynamic_slice(mix_mine, (0, g, h), (kq, 1, 1)).reshape(1, kq)

    second_f = second_blocks.astype(F32)

    source = inputs.astype(F32)
    slope_in = jax.nn.sigmoid(gate_in * source)
    gated = (source * slope_in).astype(BF16)
    mixed_first = jnp.dot(first_blocks[0], gated, preferred_element_type=F32).astype(BF16)

    upstream = cotangent
    cot_arrived = exchange([lane_chunk(upstream, t, kq) for t in chunk_of], "ch")
    act_grad_out = [
        sum(
            cot_arrived[k].astype(F32) * coefficient(chunk_of[p], origin_of[k])
            for k in range(m)
        ).astype(BF16)
        for p in range(m)
    ]
    act_grad_back = exchange(act_grad_out, "ch")
    act_grad = place_chunks(act_grad_back, [t * kq for t in origin_of], upstream)

    first_arrived = swap(split_rows(mixed_first, n), "seq")
    second_out = jnp.einsum(
        "cea,acd->ecd", second_f, first_arrived.astype(F32)
    ).astype(BF16)
    returned = swap(second_out, "seq").reshape(rows, width).astype(F32)
    slope_out = jax.nn.sigmoid(gate_out * source)
    hidden = (source + returned * slope_out).astype(BF16)
    pre_act = jnp.dot(hidden, channel_blocks[0], preferred_element_type=F32)
    activated = jax.nn.gelu(pre_act).astype(BF16)

    act_arrived = exchange([lane_chunk(activated, t, kq) for t in chunk_of], "ch")
    added_out = [
        sum(
            act_arrived[k].astype(F32) * coefficient(origin_of[k], chunk_of[p])
            for k in range(m)
        ).astype(BF16)
        for p in range(m)
    ]
    added_back = exchange(added_out, "ch")

    pre_grad = jax.vjp(jax.nn.gelu, pre_act)[1](act_grad.astype(F32))[0].astype(BF16)
    back_term = jnp.dot(pre_grad, channel_blocks[0].T, preferred_element_type=F32)
    hidden_grad = (upstream.astype(F32) + back_term).astype(BF16)
    channel_part = jnp.dot(hidden.T, pre_grad, preferred_element_type=F32)

    grad_flat = hidden_grad.astype(F32)
    gated_grad = (grad_flat * slope_out).astype(BF16)
    grad_arrived = swap(split_rows(gated_grad, n), "seq")
    first_out = jnp.einsum(
        "cea,ecd->acd", second_f, grad_arrived.astype(F32)
    ).astype(BF16)
    first_grad = swap(first_out, "seq").reshape(rows, width)
    first_grad, channel_part = lax.optimization_barrier((first_grad, channel_part))
    block_part = jnp.dot(first_grad, gated.T, preferred_element_type=F32)
    cq = block_part.shape[0] // m
    block_arrived = exchange(
        [lax.dynamic_slice_in_dim(block_part, t * cq, cq, 0).astype(BF16) for t in chunk_of],
        "ch",
    )
    first_block, added_back = lax.optimization_barrier((block_arrived[1], added_back))
    block_arrived[1] = first_block
    block_grad = sum(part.astype(F32) for part in block_arrived)[None]
    outputs = place_chunks(
        [
            (lane_chunk(hidden, t, kq).astype(F32) + part.astype(F32)).astype(BF16)
            for t, part in zip(origin_of, added_back)
        ],
        [t * kq for t in origin_of],
        hidden,
    )
    channel_arrived = swap(split_rows(channel_part, n).astype(BF16), "seq")
    channel_grad = jnp.sum(channel_arrived.astype(F32), axis=0)[None]

    spread = jnp.dot(first_blocks[0].T, first_grad, preferred_element_type=F32)
    input_grad = grad_flat + spread * (slope_in + gate_in * source * slope_in * (1.0 - slope_in))
    input_grad = input_grad + grad_flat * returned * slope_out * (1.0 - slope_out) * gate_out
    return (outputs, input_grad.astype(BF16), channel_grad, block_grad)


def solution(mesh):
    placed = (
        P("seq", "ch"),
        P("ch"),
        P("ch"),
        P("seq", None, None),
        P("seq", None, None),
        P("ch", None, None),
        P(),
        P("seq", "ch"),
    )
    return jax.shard_map(
        on_device,
        mesh=mesh,
        in_specs=placed,
        out_specs=(P("seq", "ch"), P("seq", "ch"), P("ch", "seq", None), P("seq", "ch", None)),
        check_vma=False,
    )
```
